512 devices in a mesh: seq: 64 (over x, z), head: 8 (over y, core).
Axes of the slice: x: 4, y: 4, z: 16, core: 2. Of those that a mesh axis runs over, the one named last changes fastest.
Arguments:
- queries: bfloat16 [8192, 4096], P('seq', 'head'), may hold values from -6 to 6
- keys: bfloat16 [8192, 4096], P('seq', 'head'), may hold values from -6 to 6
- values: bfloat16 [8192, 4096], P('seq', 'head'), may hold values from -6 to 6
- log_decay: float32 [8192, 32], P('seq', 'head'), may hold values from -0.75 to 0
- norm_gain: float32 [4096], P('head'), may hold values from 0.1 to 1.9
- out_weight: bfloat16 [4096, 4096], P('head'), may hold values from -0.125 to 0.125
- steer_ids: int32 [8192], P('seq'), may hold values from 0 to 15
- steer_table: bfloat16 [16, 4096], P(None, 'head'), may hold values from -3 to 3
Outputs:
- layer_out: bfloat16 [8192, 4096], P('seq', 'head')
The draws below stay inside these ranges and needn't reach their ends.
All inputs are finite; a program needn't handle non-finite values.
Results may differ from the reference program's by a relative error of at most 0.0052.
Values sent between devices are 32-bit elements; how exact they have to be, the bound alone decides.
No kernel may reach another device: no remote copies, remote signals or barrier semaphores. Data moves between devices by JAX's collectives and lax.ppermute only.
A program may use at most 64 MiB of HBM per device.

```python
import math
import jax
import jax.numpy as jnp
from jax import lax

D = 4096
HEADS = 32
HEAD_DIM = 128
SPAN = 128
NSTEER = 16
TOKENS = 8192


def draw_log_decay(key, part):
    keys_all = jax.random.split(jax.random.fold_in(key, 7), 6)
    share = 0.5
    fast = jax.random.uniform(keys_all[0], (HEADS,)) < share
    fast_rate = -1.0 / jax.random.uniform(keys_all[1], (HEADS,), minval=30.0, maxval=50.0)
    slow_rate = math.log(0.7) / TOKENS * jax.random.uniform(keys_all[2], (HEADS,), minval=0.3, maxval=1.0)
    base = jnp.where(fast, fast_rate, slow_rate)
    rough = jax.random.uniform(keys_all[3], (TOKENS, HEADS), minval=0.5, maxval=1.5)
    spots = jax.random.randint(keys_all[4], (2,), 0, TOKENS)
    places = jnp.arange(TOKENS, dtype=jnp.int32)
    struck = jnp.any(places[:, None] == spots[None, :], axis=1)
    depth = jnp.log(jax.random.uniform(keys_all[5], (TOKENS, HEADS), minval=0.5, maxval=0.8))
    result = base[None, :] * rough + jnp.where(struck[:, None], depth, 0.0)
    return result.astype(jnp.float32)


def set_ends(entries, stream_key, smallest, top_value):
    index_at = [jax.random.randint(jax.random.fold_in(stream_key, axis), (), 0, length) for axis, length in enumerate(entries.shape)]
    main_axis = entries.shape.index(max(entries.shape))
    neighbour = index_at[:main_axis] + [(index_at[main_axis] + 1) % entries.shape[main_axis]] + index_at[main_axis + 1:]
    return entries.at[tuple(index_at)].set(smallest).at[tuple(neighbour)].set(top_value)


def with_spikes(values, key, source, target, blocks, factor):
    def block_of(axis_at):
        return (jnp.arange(values.shape[axis_at]) // (values.shape[axis_at] // blocks)).reshape((-1,) + (1,) * (values.ndim - 1 - axis_at))

    near = jax.random.permutation(key, blocks)[block_of(target)]
    far = (block_of(target) + blocks // 2) % blocks
    return jnp.where((block_of(source) == near) | (block_of(source) == far), factor * values, values)


def shard_levels(stream_key, shape, shards, low, top_value):
    def one(axis_at, blocks):
        draws = jax.random.uniform(jax.random.fold_in(jax.random.fold_in(stream_key, 6), axis_at), (blocks,), jnp.float32, low / len(shards), top_value / len(shards))
        return jnp.repeat(jnp.exp(draws), shape[axis_at] // blocks).reshape((-1,) + (1,) * (len(shape) - axis_at - 1))

    loudness = one(*shards[0])
    for cut in shards[1:]:
        loudness = loudness * one(*cut)
    return loudness


def gaussian(own_key, dims, width, limit, cuts=(), held_as=jnp.bfloat16):
    values = width * jax.random.normal(own_key, dims, jnp.float32)
    if cuts:
        values = values * shard_levels(own_key, dims, cuts, -0.22, 0.18)
    return jnp.clip(values, -limit, limit).astype(held_as)


def gaussian_with(key, dims, deviation, most, shards, heavy, held_as=jnp.bfloat16):
    values = deviation * jax.random.normal(key, dims, jnp.float32)
    if shards:
        values = values * shard_levels(key, dims, shards, -0.22, 0.18)
    return jnp.clip(with_spikes(values, jax.random.fold_in(key, 3), *heavy), -most, most).astype(held_as)


def setup_inputs(seed: int = 0) -> dict:
    key_of = jax.random.split(jax.random.key(seed), 9)
    queries = gaussian(key_of[0], (TOKENS, HEADS * HEAD_DIM), 1.0, 6.0, ((0, 64), (1, 8)))
    keys = gaussian(key_of[1], (TOKENS, HEADS * HEAD_DIM), 1.0, 6.0, ((0, 64), (1, 8)))
    values = gaussian(key_of[2], (TOKENS, HEADS * HEAD_DIM), 1.0, 6.0, ((0, 64), (1, 8)))
    log_decay = draw_log_decay(jax.random.fold_in(key_of[8], 71), 0)
    norm_gain = jnp.clip(1.0 + 0.18 * jax.random.normal(key_of[4], (HEADS * HEAD_DIM,), jnp.float32), 0.1, 1.9)
    out_weight = gaussian_with(key_of[5], (HEADS * HEAD_DIM, D), (HEADS * HEAD_DIM) ** -0.5, 0.125, ((0, 8),), (0, 1, 8, 2.0))
    steer_ids = set_ends(jax.random.randint(key_of[6], (TOKENS,), 0, NSTEER), jax.random.fold_in(key_of[6], 1), 0, NSTEER - 1).astype(jnp.int32)
    steer_table = gaussian(key_of[7], (NSTEER, D), 0.5, 3.0, ((1, 8),))
    return dict(queries=queries, keys=keys, values=values, log_decay=log_decay, norm_gain=norm_gain, out_weight=out_weight, steer_ids=steer_ids, steer_table=steer_table)


def block_step(state, inputs):
    query, key_blk, value_blk, decay = inputs
    cum = jnp.cumsum(decay, axis=1)
    size = decay.shape[1]
    rows = lax.broadcasted_iota(jnp.int32, (size, size), 0)
    cols = lax.broadcasted_iota(jnp.int32, (size, size), 1)
    lower = (cols <= rows)[None]
    scores = jnp.einsum('hte,hse->hts', query.astype(jnp.float32), key_blk.astype(jnp.float32))
    diffs = jnp.where(lower, cum[:, :, None] - cum[:, None, :], 0.0)
    block_weights = jnp.where(lower, jnp.exp(diffs), 0.0) * scores
    block_weights = block_weights.astype(jnp.bfloat16)
    intra = jnp.einsum('hts,hse->hte', block_weights.astype(jnp.float32), value_blk.astype(jnp.float32))
    inter = jnp.exp(cum)[:, :, None] * jnp.einsum('hte,hef->htf', query.astype(jnp.float32), state, precision=lax.Precision.HIGHEST)
    total = cum[:, -1]
    scaled_keys = key_blk.astype(jnp.float32) * jnp.exp(total[:, None] - cum)[:, :, None]
    update = jnp.einsum('hse,hsf->hef', scaled_keys, value_blk.astype(jnp.float32), precision=lax.Precision.HIGHEST)
    new_state = jnp.exp(total)[:, None, None] * state + update
    return (new_state, intra + inter)

def reference(queries, keys, values, log_decay, norm_gain, out_weight, steer_ids, steer_table):
    count = TOKENS // SPAN

    def split(array):
        return array.reshape(count, SPAN, HEADS, HEAD_DIM).transpose(0, 2, 1, 3)
    decays = log_decay.reshape(count, SPAN, HEADS).transpose(0, 2, 1)
    start = jnp.zeros((HEADS, HEAD_DIM, HEAD_DIM), jnp.float32)
    final, blocks = lax.scan(block_step, start, (split(queries), split(keys), split(values), decays))
    attended = blocks.transpose(0, 2, 1, 3).reshape(TOKENS, HEADS, HEAD_DIM)
    mean_sq = lax.optimization_barrier(jnp.mean(attended * attended, axis=-1, keepdims=True))
    normed = (attended * lax.rsqrt(mean_sq + 1e-06)).reshape(TOKENS, HEADS * HEAD_DIM) * norm_gain
    normed = normed.astype(jnp.bfloat16)
    projected = jnp.dot(normed, out_weight, preferred_element_type=jnp.float32)
    onehot = (steer_ids[:, None] == jnp.arange(NSTEER, dtype=jnp.int32)[None, :]).astype(jnp.bfloat16)
    steering = jnp.dot(onehot, steer_table, preferred_element_type=jnp.float32)
    return (projected + steering).astype(jnp.bfloat16)
```

```python
import jax
import jax.numpy as jnp
import numpy as np
from jax import lax
from jax.sharding import PartitionSpec as P

SPAN = 128


def block_step(state, inputs):
    query, key_blk, value_blk, decay = inputs
    cum = jnp.cumsum(decay, axis=1)
    size = decay.shape[1]
    rows = lax.broadcasted_iota(jnp.int32, (size, size), 0)
    cols = lax.broadcasted_iota(jnp.int32, (size, size), 1)
    lower = (cols <= rows)[None]
    scores = jnp.einsum("hte,hse->hts", query, key_blk, preferred_element_type=jnp.float32)
    diffs = jnp.where(lower, cum[:, :, None] - cum[:, None, :], 0.0)
    block_weights = (jnp.where(lower, jnp.exp(diffs), 0.0) * scores).astype(jnp.bfloat16)
    intra = jnp.einsum("hts,hse->hte", block_weights, value_blk, preferred_element_type=jnp.float32)
    inter = jnp.exp(cum)[:, :, None] * jnp.einsum(
        "hte,hef->htf", query.astype(jnp.float32), state, precision=lax.Precision.HIGHEST
    )
    total = cum[:, -1]
    scaled_keys = key_blk.astype(jnp.float32) * jnp.exp(total[:, None] - cum)[:, :, None]
    update = jnp.einsum(
        "hse,hsf->hef", scaled_keys, value_blk.astype(jnp.float32), precision=lax.Precision.HIGHEST
    )
    new_state = jnp.exp(total)[:, None, None] * state + update
    return (new_state, intra + inter)


def join_memory(earlier, later):
    return (earlier[0] + later[0], jnp.exp(later[0])[:, None, None] * earlier[1] + later[1])


def scan_rounds(n):
    top = 1
    while top < n:
        top *= 2
    levels = top.bit_length() - 1
    ups = []
    for k in range(levels):
        step = 1 << k
        ups.append([(p - step, p) for p in range(2 * step - 1, n, 2 * step)])
    downs = []
    for k in range(levels - 1, -1, -1):
        step = 1 << k
        downs.append([(p - step, p) for p in range(3 * step - 1, n, 2 * step)])
    rounds = ups[:-1]
    tail = ups[-1] if ups else []
    downs = [d for d in downs if d]
    if tail and downs and all(s == tail[0][0] for s, _ in tail) and downs[0][0][0] == tail[0][0]:
        rounds.append(tail + downs[0])
        rounds.extend(downs[1:])
    else:
        if tail:
            rounds.append(tail)
        rounds.extend(downs)
    return [r for r in rounds if r]


def exclusive_scan(part, axis, n):
    place = lax.axis_index(axis)
    held = part
    before = (jnp.zeros_like(part[0]), jnp.zeros_like(part[1]))
    for pairs in scan_rounds(n):
        table = np.zeros((n,), np.bool_)
        for _, dst in pairs:
            table[dst] = True
        takes = jnp.asarray(table)[place]
        groups = []
        for pair in pairs:
            for group in groups:
                if all(pair[0] != other[0] for other in group):
                    group.append(pair)
                    break
            else:
                groups.append([pair])
        got = None
        for group in groups:
            one = (lax.ppermute(held[0], axis, group), lax.ppermute(held[1], axis, group))
            got = one if got is None else jax.tree.map(jnp.add, got, one)
        new_held = join_memory(got, held)
        new_before = join_memory(got, before)
        held = jax.tree.map(lambda a, b: jnp.where(takes, a, b), new_held, held)
        before = jax.tree.map(lambda a, b: jnp.where(takes, a, b), new_before, before)
    return before


def scatter_heads(partial, axis, n):
    rows, total_cols = partial.shape
    width = total_cols // n
    place = lax.axis_index(axis)
    if n % 2 == 0 and n > 2:
        chips = n // 2
        core = place % 2
        chip = place // 2
        blocks = partial.reshape(rows, chips, 2, width)
        keep = jnp.where(core == 0, blocks[:, :, 0], blocks[:, :, 1])
        away = jnp.where(core == 0, blocks[:, :, 1], blocks[:, :, 0])
        pairs = [(h, h ^ 1) for h in range(n)]
        mine = keep + lax.ppermute(away, axis, pairs)
        out = lax.dynamic_index_in_dim(mine, chip, 1, False)
        for shift in range(1, chips):
            send = lax.dynamic_index_in_dim(mine, (chip + shift) % chips, 1, False)
            pairs = [(2 * y + c, 2 * ((y + shift) % chips) + c) for y in range(chips) for c in range(2)]
            out = out + lax.ppermute(send, axis, pairs)
        return out
    whole = lax.psum(partial, axis)
    return lax.dynamic_slice_in_dim(whole, place * width, width, 1)


def shards(queries, keys, values, log_decay, norm_gain, out_weight, steer_ids, steer_table, seq_n, head_n):
    tok_rows, features = queries.shape
    heads_here = log_decay.shape[1]
    head_size = features // heads_here
    count = tok_rows // SPAN

    def split(array):
        return array.reshape(count, SPAN, heads_here, head_size).transpose(0, 2, 1, 3)

    decays = log_decay.reshape(count, SPAN, heads_here).transpose(0, 2, 1)
    start = jnp.zeros((heads_here, head_size, head_size), jnp.float32)
    local_memory, blocks = lax.scan(
        block_step, start, (split(queries), split(keys), split(values), decays)
    )
    device_log = jnp.sum(log_decay, axis=0)
    passed = exclusive_scan((device_log, local_memory), "seq", seq_n)
    earlier_memory = passed[1]
    running = jnp.cumsum(log_decay, axis=0)
    query_heads = queries.reshape(tok_rows, heads_here, head_size).astype(jnp.float32)
    carried = jnp.exp(running)[:, :, None] * jnp.einsum(
        "the,hef->thf", query_heads, earlier_memory, precision=lax.Precision.HIGHEST
    )
    attended = blocks.transpose(0, 2, 1, 3).reshape(tok_rows, heads_here, head_size) + carried
    mean_sq = jnp.mean(attended * attended, axis=-1, keepdims=True)
    normed = (attended * lax.rsqrt(mean_sq + 1e-06)).reshape(tok_rows, features) * norm_gain
    normed = normed.astype(jnp.bfloat16)
    partial_term = jnp.dot(normed, out_weight, preferred_element_type=jnp.float32)
    onehot = (
        steer_ids[:, None] == jnp.arange(steer_table.shape[0], dtype=jnp.int32)[None, :]
    ).astype(jnp.bfloat16)
    steering = jnp.dot(onehot, steer_table, preferred_element_type=jnp.float32)
    summed = scatter_heads(partial_term, "head", head_n)
    return (summed + steering).astype(jnp.bfloat16)


def solution(mesh):
    in_specs = (
        P("seq", "head"),
        P("seq", "head"),
        P("seq", "head"),
        P("seq", "head"),
        P("head"),
        P("head", None),
        P("seq"),
        P(None, "head"),
    )
    out_specs = P("seq", "head")
    seq_n = mesh.shape["seq"]
    head_n = mesh.shape["head"]

    def body(*args):
        return shards(*args, seq_n=seq_n, head_n=head_n)

    return jax.shard_map(body, mesh=mesh, in_specs=in_specs, out_specs=out_specs, check_vma=False)
```

```python
import jax
import jax.numpy as jnp
import numpy as np
from jax import lax
from jax.sharding import PartitionSpec as P

SPAN = 128


def block_step(state, inputs):
    query, key_blk, value_blk, decay = inputs
    cum = jnp.cumsum(decay, axis=1)
    size = decay.shape[1]
    rows = lax.broadcasted_iota(jnp.int32, (size, size), 0)
    cols = lax.broadcasted_iota(jnp.int32, (size, size), 1)
    lower = (cols <= rows)[None]
    scores = jnp.einsum("hte,hse->hts", query, key_blk, preferred_element_type=jnp.float32)
    diffs = jnp.where(lower, cum[:, :, None] - cum[:, None, :], 0.0)
    block_weights = (jnp.where(lower, jnp.exp(diffs), 0.0) * scores).astype(jnp.bfloat16)
    intra = jnp.einsum("hts,hse->hte", block_weights, value_blk, preferred_element_type=jnp.float32)
    inter = jnp.exp(cum)[:, :, None] * jnp.einsum(
        "hte,hef->htf", query.astype(jnp.float32), state, precision=lax.Precision.HIGHEST
    )
    total = cum[:, -1]
    scaled_keys = key_blk.astype(jnp.float32) * jnp.exp(total[:, None] - cum)[:, :, None]
    update = jnp.einsum(
        "hse,hsf->hef", scaled_keys, value_blk.astype(jnp.float32), precision=lax.Precision.HIGHEST
    )
    new_state = jnp.exp(total)[:, None, None] * state + update
    return (new_state, intra + inter)


def pack(log_total, memory):
    heads, rows, cols = memory.shape
    extra = jnp.broadcast_to(log_total[:, None, None], (heads, 8, cols))
    return jnp.concatenate([memory, extra], axis=1)


def join(earlier, later):
    rows = earlier.shape[1] - 8
    row = lax.broadcasted_iota(jnp.int32, earlier.shape, 1)
    scale = jnp.where(row < rows, jnp.exp(later[:, rows:rows + 1, :]), 1.0)
    return scale * earlier + later


def bk_rounds(n):
    top = 1
    while top < n:
        top *= 2
    levels = top.bit_length() - 1
    ups = []
    for k in range(levels):
        step = 1 << k
        ups.append([(p - step, p) for p in range(2 * step - 1, n, 2 * step)])
    downs = []
    for k in range(levels - 1, -1, -1):
        step = 1 << k
        downs.append([(p - step, p) for p in range(3 * step - 1, n, 2 * step)])
    rounds = ups[:-1]
    tail = ups[-1] if ups else []
    downs = [d for d in downs if d]
    if tail and downs and all(s == tail[0][0] for s, _ in tail) and downs[0][0][0] == tail[0][0]:
        rounds.append(tail + downs[0])
        rounds.extend(downs[1:])
    else:
        if tail:
            rounds.append(tail)
        rounds.extend(downs)
    return [r for r in rounds if r]


def unique_sources(pairs):
    groups = []
    for pair in pairs:
        for group in groups:
            if all(pair[0] != other[0] for other in group):
                group.append(pair)
                break
        else:
            groups.append([pair])
    return groups


def receive(value, axis, pairs):
    got = None
    for group in unique_sources(pairs):
        one = lax.ppermute(value, axis, group)
        got = one if got is None else got + one
    return got


def exclusive_scan(part, axis, lines, width):
    held = part
    before = jnp.zeros_like(part)
    after = part
    for pairs in bk_rounds(width):
        fwd = [(l * width + s, l * width + d) for l in range(lines) for s, d in pairs]
        bwd = [(l * width + width - 1 - s, l * width + width - 1 - d) for l in range(lines) for s, d in pairs]
        got = receive(held, axis, fwd)
        back = receive(after, axis, bwd)
        held = join(got, held)
        before = join(got, before)
        after = join(after, back)
    total = join(before, after)
    if lines == 1:
        return before
    earlier = None
    for shift in range(lines - 1, 0, -1):
        pairs = [((l - shift) * width + p, l * width + p) for l in range(shift, lines) for p in range(width)]
        got = lax.ppermute(total, axis, pairs)
        earlier = got if earlier is None else join(earlier, got)
    return join(earlier, before)


def scatter_heads(partial, axis, n):
    rows, total_cols = partial.shape
    width = total_cols // n
    place = lax.axis_index(axis)
    if n % 2 == 0 and n > 2:
        chips = n // 2
        core = place % 2
        chip = place // 2
        blocks = partial.reshape(rows, chips, 2, width)
        keep = jnp.where(core == 0, blocks[:, :, 0], blocks[:, :, 1])
        away = jnp.where(core == 0, blocks[:, :, 1], blocks[:, :, 0])
        pairs = [(h, h ^ 1) for h in range(n)]
        mine = keep + lax.ppermute(away, axis, pairs)
        out = lax.dynamic_index_in_dim(mine, chip, 1, False)
        for shift in range(1, chips):
            send = lax.dynamic_index_in_dim(mine, (chip + shift) % chips, 1, False)
            pairs = [(2 * y + c, 2 * ((y + shift) % chips) + c) for y in range(chips) for c in range(2)]
            out = out + lax.ppermute(send, axis, pairs)
        return out
    whole = lax.psum(partial, axis)
    return lax.dynamic_slice_in_dim(whole, place * width, width, 1)


def shards(queries, keys, values, log_decay, norm_gain, out_weight, steer_ids, steer_table, seq_n, seq_width, head_n):
    tok_rows, features = queries.shape
    heads_here = log_decay.shape[1]
    head_size = features // heads_here
    count = tok_rows // SPAN

    def split(array):
        return array.reshape(count, SPAN, heads_here, head_size).transpose(0, 2, 1, 3)

    decays = log_decay.reshape(count, SPAN, heads_here).transpose(0, 2, 1)
    start = jnp.zeros((heads_here, head_size, head_size), jnp.float32)
    local_memory, blocks = lax.scan(
        block_step, start, (split(queries), split(keys), split(values), decays)
    )
    device_log = jnp.sum(log_decay, axis=0)
    lines, width = seq_n // seq_width, seq_width
    passed = exclusive_scan(pack(device_log, local_memory), "seq", lines, width)
    earlier_memory = passed[:, :head_size, :]
    running = jnp.cumsum(log_decay, axis=0)
    query_heads = queries.reshape(tok_rows, heads_here, head_size).astype(jnp.float32)
    carried = jnp.exp(running)[:, :, None] * jnp.einsum(
        "the,hef->thf", query_heads, earlier_memory, precision=lax.Precision.HIGHEST
    )
    attended = blocks.transpose(0, 2, 1, 3).reshape(tok_rows, heads_here, head_size) + carried
    mean_sq = jnp.mean(attended * attended, axis=-1, keepdims=True)
    normed = (attended * lax.rsqrt(mean_sq + 1e-06)).reshape(tok_rows, features) * norm_gain
    normed = normed.astype(jnp.bfloat16)
    partial_term = jnp.dot(normed, out_weight, preferred_element_type=jnp.float32)
    onehot = (
        steer_ids[:, None] == jnp.arange(steer_table.shape[0], dtype=jnp.int32)[None, :]
    ).astype(jnp.bfloat16)
    steering = jnp.dot(onehot, steer_table, preferred_element_type=jnp.float32)
    summed = scatter_heads(partial_term, "head", head_n)
    return (summed + steering).astype(jnp.bfloat16)


def line_width(mesh):
    devices = np.moveaxis(mesh.devices, mesh.axis_names.index("seq"), 0)
    order = devices.reshape(devices.shape[0], -1)[:, 0]
    n = len(order)
    firsts = [tuple(getattr(d, "coords", (0,)))[0] for d in order]
    width = 1
    while width < n and firsts[width] == firsts[0]:
        width += 1
    if n % width or width & (width - 1):
        return n
    return width


def solution(mesh):
    in_specs = (
        P("seq", "head"),
        P("seq", "head"),
        P("seq", "head"),
        P("seq", "head"),
        P("head"),
        P("head", None),
        P("seq"),
        P(None, "head"),
    )
    out_specs = P("seq", "head")
    seq_n = mesh.shape["seq"]
    head_n = mesh.shape["head"]
    seq_width = line_width(mesh)

    def body(*args):
        return shards(*args, seq_n=seq_n, seq_width=seq_width, head_n=head_n)

    return jax.shard_map(body, mesh=mesh, in_specs=in_specs, out_specs=out_specs, check_vma=False)
```

```python
import jax
import jax.numpy as jnp
import numpy as np
from jax import lax
from jax.sharding import PartitionSpec as P

SPAN = 128


def block_step(state, inputs):
    query, key_blk, value_blk, decay = inputs
    cum = jnp.cumsum(decay, axis=1)
    size = decay.shape[1]
    rows = lax.broadcasted_iota(jnp.int32, (size, size), 0)
    cols = lax.broadcasted_iota(jnp.int32, (size, size), 1)
    lower = (cols <= rows)[None]
    scores = jnp.einsum("hte,hse->hts", query, key_blk, preferred_element_type=jnp.float32)
    diffs = jnp.where(lower, cum[:, :, None] - cum[:, None, :], 0.0)
    block_weights = (jnp.where(lower, jnp.exp(diffs), 0.0) * scores).astype(jnp.bfloat16)
    intra = jnp.einsum("hts,hse->hte", block_weights, value_blk, preferred_element_type=jnp.float32)
    inter = jnp.exp(cum)[:, :, None] * jnp.einsum(
        "hte,hef->htf", query.astype(jnp.float32), state, precision=lax.Precision.HIGHEST
    )
    total = cum[:, -1]
    scaled_keys = key_blk.astype(jnp.float32) * jnp.exp(total[:, None] - cum)[:, :, None]
    update = jnp.einsum(
        "hse,hsf->hef", scaled_keys, value_blk.astype(jnp.float32), precision=lax.Precision.HIGHEST
    )
    new_state = jnp.exp(total)[:, None, None] * state + update
    return (new_state, intra + inter)


def pack(log_total, memory):
    heads, rows, cols = memory.shape
    extra = jnp.broadcast_to(log_total[:, None, None], (heads, 8, cols))
    return jnp.concatenate([memory, extra], axis=1)


def join(earlier, later):
    rows = earlier.shape[1] - 8
    row = lax.broadcasted_iota(jnp.int32, earlier.shape, 1)
    scale = jnp.where(row < rows, jnp.exp(later[:, rows:rows + 1, :]), 1.0)
    return scale * earlier + later


def bk_rounds(n):
    top = 1
    while top < n:
        top *= 2
    levels = top.bit_length() - 1
    ups = []
    for k in range(levels):
        step = 1 << k
        ups.append([(p - step, p) for p in range(2 * step - 1, n, 2 * step)])
    downs = []
    for k in range(levels - 1, -1, -1):
        step = 1 << k
        downs.append([(p - step, p) for p in range(3 * step - 1, n, 2 * step)])
    rounds = ups[:-1]
    tail = ups[-1] if ups else []
    downs = [d for d in downs if d]
    if tail and downs and all(s == tail[0][0] for s, _ in tail) and downs[0][0][0] == tail[0][0]:
        rounds.append(tail + downs[0])
        rounds.extend(downs[1:])
    else:
        if tail:
            rounds.append(tail)
        rounds.extend(downs)
    return [r for r in rounds if r]


def unique_sources(pairs):
    groups = []
    for pair in pairs:
        for group in groups:
            if all(pair[0] != other[0] for other in group):
                group.append(pair)
                break
        else:
            groups.append([pair])
    return groups


def receive(value, axis, pairs):
    got = None
    for group in unique_sources(pairs):
        one = lax.ppermute(value, axis, group)
        got = one if got is None else got + one
    return got


def member(position, spots):
    bits = 0
    for spot in spots:
        bits |= 1 << spot
    return ((jnp.int32(bits) >> position) & 1) == 1


def exclusive_scan(part, axis, lines, width):
    pos = lax.axis_index(axis) % width
    held = part
    before = jnp.zeros_like(part)
    after = part
    for pairs in bk_rounds(width):
        fwd_groups = unique_sources(pairs)
        ahead = None
        behind = None
        for group in fwd_groups:
            back = [(width - 1 - s, width - 1 - d) for s, d in group]
            both = group + back
            assert len({s for s, _ in both}) == len(both) and len({d for _, d in both}) == len(both)
            send = jnp.where(member(pos, [s for s, _ in group]), held, after)
            full = [(l * width + s, l * width + d) for l in range(lines) for s, d in both]
            got = lax.ppermute(send, axis, full)
            one_ahead = jnp.where(member(pos, [d for _, d in group]), got, 0.0)
            one_behind = jnp.where(member(pos, [d for _, d in back]), got, 0.0)
            ahead = one_ahead if ahead is None else ahead + one_ahead
            behind = one_behind if behind is None else behind + one_behind
        held = join(ahead, held)
        before = join(ahead, before)
        after = join(after, behind)
    total = join(before, after)
    if lines == 1:
        return before
    earlier = None
    for shift in range(lines - 1, 0, -1):
        pairs = [((l - shift) * width + p, l * width + p) for l in range(shift, lines) for p in range(width)]
        got = lax.ppermute(total, axis, pairs)
        earlier = got if earlier is None else join(earlier, got)
    return join(earlier, before)


def scatter_heads(partial, axis, n):
    rows, total_cols = partial.shape
    width = total_cols // n
    place = lax.axis_index(axis)
    if n % 2 == 0 and n > 2:
        chips = n // 2
        core = place % 2
        chip = place // 2
        blocks = partial.reshape(rows, chips, 2, width)
        keep = jnp.where(core == 0, blocks[:, :, 0], blocks[:, :, 1])
        away = jnp.where(core == 0, blocks[:, :, 1], blocks[:, :, 0])
        pairs = [(h, h ^ 1) for h in range(n)]
        mine = keep + lax.ppermute(away, axis, pairs)
        out = lax.dynamic_index_in_dim(mine, chip, 1, False)
        for shift in range(1, chips):
            send = lax.dynamic_index_in_dim(mine, (chip + shift) % chips, 1, False)
            pairs = [(2 * y + c, 2 * ((y + shift) % chips) + c) for y in range(chips) for c in range(2)]
            out = out + lax.ppermute(send, axis, pairs)
        return out
    whole = lax.psum(partial, axis)
    return lax.dynamic_slice_in_dim(whole, place * width, width, 1)


def shards(queries, keys, values, log_decay, norm_gain, out_weight, steer_ids, steer_table, seq_n, seq_width, head_n):
    tok_rows, features = queries.shape
    heads_here = log_decay.shape[1]
    head_size = features // heads_here
    count = tok_rows // SPAN

    def split(array):
        return array.reshape(count, SPAN, heads_here, head_size).transpose(0, 2, 1, 3)

    decays = log_decay.reshape(count, SPAN, heads_here).transpose(0, 2, 1)
    start = jnp.zeros((heads_here, head_size, head_size), jnp.float32)
    local_memory, blocks = lax.scan(
        block_step, start, (split(queries), split(keys), split(values), decays)
    )
    device_log = jnp.sum(log_decay, axis=0)
    lines, width = seq_n // seq_width, seq_width
    passed = exclusive_scan(pack(device_log, local_memory), "seq", lines, width)
    earlier_memory = passed[:, :head_size, :]
    running = jnp.cumsum(log_decay, axis=0)
    query_heads = queries.reshape(tok_rows, heads_here, head_size).astype(jnp.float32)
    carried = jnp.exp(running)[:, :, None] * jnp.einsum(
        "the,hef->thf", query_heads, earlier_memory, precision=lax.Precision.HIGHEST
    )
    attended = blocks.transpose(0, 2, 1, 3).reshape(tok_rows, heads_here, head_size) + carried
    mean_sq = jnp.mean(attended * attended, axis=-1, keepdims=True)
    normed = (attended * lax.rsqrt(mean_sq + 1e-06)).reshape(tok_rows, features) * norm_gain
    normed = normed.astype(jnp.bfloat16)
    partial_term = lax.optimization_barrier(jnp.dot(normed, out_weight, preferred_element_type=jnp.float32))
    onehot = (
        steer_ids[:, None] == jnp.arange(steer_table.shape[0], dtype=jnp.int32)[None, :]
    ).astype(jnp.bfloat16)
    steering = jnp.dot(onehot, steer_table, preferred_element_type=jnp.float32)
    summed = scatter_heads(partial_term, "head", head_n)
    return (summed + steering).astype(jnp.bfloat16)


def line_width(mesh):
    devices = np.moveaxis(mesh.devices, mesh.axis_names.index("seq"), 0)
    order = devices.reshape(devices.shape[0], -1)[:, 0]
    n = len(order)
    firsts = [tuple(getattr(d, "coords", (0,)))[0] for d in order]
    width = 1
    while width < n and firsts[width] == firsts[0]:
        width += 1
    if n % width or width & (width - 1):
        return n
    return width


def solution(mesh):
    in_specs = (
        P("seq", "head"),
        P("seq", "head"),
        P("seq", "head"),
        P("seq", "head"),
        P("head"),
        P("head", None),
        P("seq"),
        P(None, "head"),
    )
    out_specs = P("seq", "head")
    seq_n = mesh.shape["seq"]
    head_n = mesh.shape["head"]
    seq_width = line_width(mesh)

    def body(*args):
        return shards(*args, seq_n=seq_n, seq_width=seq_width, head_n=head_n)

    return jax.shard_map(body, mesh=mesh, in_specs=in_specs, out_specs=out_specs, check_vma=False)
```

```python
import jax
import jax.numpy as jnp
import numpy as np
from jax import lax
from jax.sharding import PartitionSpec as P

SPAN = 128


def block_step(state, inputs):
    query, key_blk, value_blk, decay = inputs
    cum = jnp.cumsum(decay, axis=1)
    size = decay.shape[1]
    rows = lax.broadcasted_iota(jnp.int32, (size, size), 0)
    cols = lax.broadcasted_iota(jnp.int32, (size, size), 1)
    lower = (cols <= rows)[None]
    scores = jnp.einsum("hte,hse->hts", query, key_blk, preferred_element_type=jnp.float32)
    diffs = jnp.where(lower, cum[:, :, None] - cum[:, None, :], 0.0)
    block_weights = (jnp.where(lower, jnp.exp(diffs), 0.0) * scores).astype(jnp.bfloat16)
    intra = jnp.einsum("hts,hse->hte", block_weights, value_blk, preferred_element_type=jnp.float32)
    inter = jnp.exp(cum)[:, :, None] * jnp.einsum(
        "hte,hef->htf", query.astype(jnp.float32), state, precision=lax.Precision.HIGHEST
    )
    total = cum[:, -1]
    scaled_keys = key_blk.astype(jnp.float32) * jnp.exp(total[:, None] - cum)[:, :, None]
    update = jnp.einsum(
        "hse,hsf->hef", scaled_keys, value_blk.astype(jnp.float32), precision=lax.Precision.HIGHEST
    )
    new_state = jnp.exp(total)[:, None, None] * state + update
    return (new_state, intra + inter)


def pack(log_total, memory):
    heads, rows, cols = memory.shape
    extra = jnp.broadcast_to(log_total[:, None, None], (heads, 8, cols))
    return jnp.concatenate([memory, extra], axis=1)


def join(earlier, later):
    rows = earlier.shape[1] - 8
    row = lax.broadcasted_iota(jnp.int32, earlier.shape, 1)
    scale = jnp.where(row < rows, jnp.exp(later[:, rows:rows + 1, :]), 1.0)
    return scale * earlier + later


def bk_rounds(n):
    top = 1
    while top < n:
        top *= 2
    levels = top.bit_length() - 1
    ups = []
    for k in range(levels):
        step = 1 << k
        ups.append([(p - step, p) for p in range(2 * step - 1, n, 2 * step)])
    downs = []
    for k in range(levels - 1, -1, -1):
        step = 1 << k
        downs.append([(p - step, p) for p in range(3 * step - 1, n, 2 * step)])
    rounds = ups[:-1]
    tail = ups[-1] if ups else []
    downs = [d for d in downs if d]
    if tail and downs and all(s == tail[0][0] for s, _ in tail) and downs[0][0][0] == tail[0][0]:
        rounds.append(tail + downs[0])
        rounds.extend(downs[1:])
    else:
        if tail:
            rounds.append(tail)
        rounds.extend(downs)
    return [r for r in rounds if r]


def unique_sources(pairs):
    groups = []
    for pair in pairs:
        for group in groups:
            if all(pair[0] != other[0] for other in group):
                group.append(pair)
                break
        else:
            groups.append([pair])
    return groups


def receive(value, axis, pairs):
    got = None
    for group in unique_sources(pairs):
        one = lax.ppermute(value, axis, group)
        got = one if got is None else got + one
    return got


def member(position, spots):
    bits = 0
    for spot in spots:
        bits |= 1 << spot
    return ((jnp.int32(bits) >> position) & 1) == 1


def exclusive_scan(part, axis, lines, width):
    pos = lax.axis_index(axis) % width
    held = part
    before = jnp.zeros_like(part)
    after = part
    for pairs in bk_rounds(width):
        fwd_groups = unique_sources(pairs)
        ahead = None
        behind = None
        for group in fwd_groups:
            back = [(width - 1 - s, width - 1 - d) for s, d in group]
            both = group + back
            assert len({s for s, _ in both}) == len(both) and len({d for _, d in both}) == len(both)
            send = jnp.where(member(pos, [s for s, _ in group]), held, after)
            full = [(l * width + s, l * width + d) for l in range(lines) for s, d in both]
            got = lax.ppermute(send, axis, full)
            one_ahead = jnp.where(member(pos, [d for _, d in group]), got, 0.0)
            one_behind = jnp.where(member(pos, [d for _, d in back]), got, 0.0)
            ahead = one_ahead if ahead is None else ahead + one_ahead
            behind = one_behind if behind is None else behind + one_behind
        held = join(ahead, held)
        before = join(ahead, before)
        after = join(after, behind)
    total = join(before, after)
    if lines == 1:
        return before
    earlier = None
    for shift in range(lines - 1, 0, -1):
        pairs = [((l - shift) * width + p, l * width + p) for l in range(shift, lines) for p in range(width)]
        got = lax.ppermute(total, axis, pairs)
        earlier = got if earlier is None else join(earlier, got)
    return join(earlier, before)


def scatter_heads(partial, axis, n):
    rows, total_cols = partial.shape
    width = total_cols // n
    place = lax.axis_index(axis)
    if n % 2 == 0 and n > 2:
        chips = n // 2
        core = place % 2
        chip = place // 2

        def block(index):
            return lax.dynamic_slice_in_dim(partial, index * width, width, 1)

        keep = jnp.stack([block(2 * y + core) for y in range(chips)])
        away = jnp.stack([block(2 * y + 1 - core) for y in range(chips)])
        pairs = [(h, h ^ 1) for h in range(n)]
        mine = keep + lax.ppermute(away, axis, pairs)
        out = lax.dynamic_index_in_dim(mine, chip, 0, False)
        for shift in range(1, chips):
            send = lax.dynamic_index_in_dim(mine, (chip + shift) % chips, 0, False)
            pairs = [(2 * y + c, 2 * ((y + shift) % chips) + c) for y in range(chips) for c in range(2)]
            out = out + lax.ppermute(send, axis, pairs)
        return out
    whole = lax.psum(partial, axis)
    return lax.dynamic_slice_in_dim(whole, place * width, width, 1)


def shards(queries, keys, values, log_decay, norm_gain, out_weight, steer_ids, steer_table, seq_n, seq_width, head_n):
    tok_rows, features = queries.shape
    heads_here = log_decay.shape[1]
    head_size = features // heads_here
    count = tok_rows // SPAN

    def split(array):
        return array.reshape(count, SPAN, heads_here, head_size).transpose(0, 2, 1, 3)

    decays = log_decay.reshape(count, SPAN, heads_here).transpose(0, 2, 1)
    start = jnp.zeros((heads_here, head_size, head_size), jnp.float32)
    local_memory, blocks = lax.scan(
        block_step, start, (split(queries), split(keys), split(values), decays)
    )
    device_log = jnp.sum(log_decay, axis=0)
    lines, width = seq_n // seq_width, seq_width
    passed = exclusive_scan(pack(device_log, local_memory), "seq", lines, width)
    earlier_memory = passed[:, :head_size, :]
    running = jnp.cumsum(log_decay, axis=0)
    query_heads = queries.reshape(tok_rows, heads_here, head_size).astype(jnp.float32)
    carried = jnp.exp(running)[:, :, None] * jnp.einsum(
        "the,hef->thf", query_heads, earlier_memory, precision=lax.Precision.HIGHEST
    )
    attended = blocks.transpose(0, 2, 1, 3).reshape(tok_rows, heads_here, head_size) + carried
    mean_sq = jnp.mean(attended * attended, axis=-1, keepdims=True)
    normed = (attended * lax.rsqrt(mean_sq + 1e-06)).reshape(tok_rows, features) * norm_gain
    normed = normed.astype(jnp.bfloat16)
    partial_term = lax.optimization_barrier(jnp.dot(normed, out_weight, preferred_element_type=jnp.float32))
    onehot = (
        steer_ids[:, None] == jnp.arange(steer_table.shape[0], dtype=jnp.int32)[None, :]
    ).astype(jnp.bfloat16)
    steering = jnp.dot(onehot, steer_table, preferred_element_type=jnp.float32)
    summed = scatter_heads(partial_term, "head", head_n)
    return (summed + steering).astype(jnp.bfloat16)


def line_width(mesh):
    devices = np.moveaxis(mesh.devices, mesh.axis_names.index("seq"), 0)
    order = devices.reshape(devices.shape[0], -1)[:, 0]
    n = len(order)
    firsts = [tuple(getattr(d, "coords", (0,)))[0] for d in order]
    width = 1
    while width < n and firsts[width] == firsts[0]:
        width += 1
    if n % width or width & (width - 1):
        return n
    return width


def solution(mesh):
    in_specs = (
        P("seq", "head"),
        P("seq", "head"),
        P("seq", "head"),
        P("seq", "head"),
        P("head"),
        P("head", None),
        P("seq"),
        P(None, "head"),
    )
    out_specs = P("seq", "head")
    seq_n = mesh.shape["seq"]
    head_n = mesh.shape["head"]
    seq_width = line_width(mesh)

    def body(*args):
        return shards(*args, seq_n=seq_n, seq_width=seq_width, head_n=head_n)

    return jax.shard_map(body, mesh=mesh, in_specs=in_specs, out_specs=out_specs, check_vma=False)
```

```python
import jax
import jax.numpy as jnp
import numpy as np
from jax import lax
from jax.sharding import PartitionSpec as P

SPAN = 128


def block_step(state, inputs):
    query, key_blk, value_blk, decay = inputs
    cum = jnp.cumsum(decay, axis=1)
    size = decay.shape[1]
    rows = lax.broadcasted_iota(jnp.int32, (size, size), 0)
    cols = lax.broadcasted_iota(jnp.int32, (size, size), 1)
    lower = (cols <= rows)[None]
    scores = jnp.einsum("hte,hse->hts", query, key_blk, preferred_element_type=jnp.float32)
    diffs = jnp.where(lower, cum[:, :, None] - cum[:, None, :], 0.0)
    block_weights = (jnp.where(lower, jnp.exp(diffs), 0.0) * scores).astype(jnp.bfloat16)
    intra = jnp.einsum("hts,hse->hte", block_weights, value_blk, preferred_element_type=jnp.float32)
    inter = jnp.exp(cum)[:, :, None] * jnp.einsum(
        "hte,hef->htf", query.astype(jnp.float32), state, precision=lax.Precision.HIGHEST
    )
    total = cum[:, -1]
    scaled_keys = key_blk.astype(jnp.float32) * jnp.exp(total[:, None] - cum)[:, :, None]
    update = jnp.einsum(
        "hse,hsf->hef", scaled_keys, value_blk.astype(jnp.float32), precision=lax.Precision.HIGHEST
    )
    new_state = jnp.exp(total)[:, None, None] * state + update
    return (new_state, intra + inter)


def pack(log_total, memory):
    heads, rows, cols = memory.shape
    extra = jnp.broadcast_to(log_total[:, None, None], (heads, 8, cols))
    return jnp.concatenate([memory, extra], axis=1)


def join(earlier, later):
    rows = earlier.shape[1] - 8
    row = lax.broadcasted_iota(jnp.int32, earlier.shape, 1)
    scale = jnp.where(row < rows, jnp.exp(later[:, rows:rows + 1, :]), 1.0)
    return scale * earlier + later


def member(position, spots):
    bits = 0
    for spot in spots:
        bits |= 1 << spot
    return ((jnp.int32(bits) >> position) & 1) == 1


def line_rounds(width):
    levels = width.bit_length() - 1
    rounds = []

    def both(pairs):
        fwd = [(s, d, True, True) for s, d in pairs]
        bwd = [(width - 1 - s, width - 1 - d, False, False) for s, d in pairs]
        return fwd + bwd

    for k in range(levels - 1):
        step = 1 << k
        rounds.append(both([(p - step, p) for p in range(2 * step - 1, width, 2 * step)]))
    if width >= 2:
        close = [(0, width - 1, False, True), (width - 1, 0, True, False)]
        if levels >= 2:
            step = width // 4
            close += both([(width // 2 - 1, 3 * step - 1)])
        rounds.append(close)
    for k in range(levels - 3, -1, -1):
        step = 1 << k
        rounds.append(both([(p - step, p) for p in range(3 * step - 1, width, 2 * step)]))
    return rounds


def exclusive_scan(part, axis, lines, width):
    pos = lax.axis_index(axis) % width
    held = part
    before = jnp.zeros_like(part)
    after = part
    for entries in line_rounds(width):
        assert len({e[0] for e in entries}) == len(entries) and len({e[1] for e in entries}) == len(entries)
        send = jnp.where(member(pos, [e[0] for e in entries if e[2]]), held, after)
        full = [(l * width + e[0], l * width + e[1]) for l in range(lines) for e in entries]
        got = lax.ppermute(send, axis, full)
        ahead = jnp.where(member(pos, [e[1] for e in entries if e[3]]), got, 0.0)
        behind = jnp.where(member(pos, [e[1] for e in entries if not e[3]]), got, 0.0)
        held = join(ahead, held)
        before = join(ahead, before)
        after = join(after, behind)
    total = join(before, after)
    if lines == 1:
        return before
    earlier = None
    for shift in range(lines - 1, 0, -1):
        pairs = [((l - shift) * width + p, l * width + p) for l in range(shift, lines) for p in range(width)]
        got = lax.ppermute(total, axis, pairs)
        earlier = got if earlier is None else join(earlier, got)
    return join(earlier, before)


def scatter_heads(partial, axis, n):
    rows, total_cols = partial.shape
    width = total_cols // n
    place = lax.axis_index(axis)
    if n % 2 == 0 and n > 2:
        chips = n // 2
        core = place % 2
        chip = place // 2

        def block(index):
            return lax.dynamic_slice_in_dim(partial, index * width, width, 1)

        keep = jnp.stack([block(2 * y + core) for y in range(chips)])
        away = jnp.stack([block(2 * y + 1 - core) for y in range(chips)])
        pairs = [(h, h ^ 1) for h in range(n)]
        mine = keep + lax.ppermute(away, axis, pairs)
        out = lax.dynamic_index_in_dim(mine, chip, 0, False)
        for shift in range(1, chips):
            send = lax.dynamic_index_in_dim(mine, (chip + shift) % chips, 0, False)
            pairs = [(2 * y + c, 2 * ((y + shift) % chips) + c) for y in range(chips) for c in range(2)]
            out = out + lax.ppermute(send, axis, pairs)
        return out
    whole = lax.psum(partial, axis)
    return lax.dynamic_slice_in_dim(whole, place * width, width, 1)


def shards(queries, keys, values, log_decay, norm_gain, out_weight, steer_ids, steer_table, seq_n, seq_width, head_n):
    tok_rows, features = queries.shape
    heads_here = log_decay.shape[1]
    head_size = features // heads_here
    count = tok_rows // SPAN

    def split(array):
        return array.reshape(count, SPAN, heads_here, head_size).transpose(0, 2, 1, 3)

    decays = log_decay.reshape(count, SPAN, heads_here).transpose(0, 2, 1)
    start = jnp.zeros((heads_here, head_size, head_size), jnp.float32)
    local_memory, blocks = lax.scan(
        block_step, start, (split(queries), split(keys), split(values), decays)
    )
    device_log = jnp.sum(log_decay, axis=0)
    lines, width = seq_n // seq_width, seq_width
    passed = exclusive_scan(pack(device_log, local_memory), "seq", lines, width)
    earlier_memory = passed[:, :head_size, :]
    running = jnp.cumsum(log_decay, axis=0)
    query_heads = queries.reshape(tok_rows, heads_here, head_size).astype(jnp.float32)
    carried = jnp.exp(running)[:, :, None] * jnp.einsum(
        "the,hef->thf", query_heads, earlier_memory, precision=lax.Precision.HIGHEST
    )
    attended = blocks.transpose(0, 2, 1, 3).reshape(tok_rows, heads_here, head_size) + carried
    mean_sq = jnp.mean(attended * attended, axis=-1, keepdims=True)
    normed = (attended * lax.rsqrt(mean_sq + 1e-06)).reshape(tok_rows, features) * norm_gain
    normed = normed.astype(jnp.bfloat16)
    partial_term = lax.optimization_barrier(jnp.dot(normed, out_weight, preferred_element_type=jnp.float32))
    onehot = (
        steer_ids[:, None] == jnp.arange(steer_table.shape[0], dtype=jnp.int32)[None, :]
    ).astype(jnp.bfloat16)
    steering = jnp.dot(onehot, steer_table, preferred_element_type=jnp.float32)
    summed = scatter_heads(partial_term, "head", head_n)
    return (summed + steering).astype(jnp.bfloat16)


def line_width(mesh):
    devices = np.moveaxis(mesh.devices, mesh.axis_names.index("seq"), 0)
    order = devices.reshape(devices.shape[0], -1)[:, 0]
    n = len(order)
    firsts = [tuple(getattr(d, "coords", (0,)))[0] for d in order]
    width = 1
    while width < n and firsts[width] == firsts[0]:
        width += 1
    if n % width or width & (width - 1):
        return n
    return width


def solution(mesh):
    in_specs = (
        P("seq", "head"),
        P("seq", "head"),
        P("seq", "head"),
        P("seq", "head"),
        P("head"),
        P("head", None),
        P("seq"),
        P(None, "head"),
    )
    out_specs = P("seq", "head")
    seq_n = mesh.shape["seq"]
    head_n = mesh.shape["head"]
    seq_width = line_width(mesh)

    def body(*args):
        return shards(*args, seq_n=seq_n, seq_width=seq_width, head_n=head_n)

    return jax.shard_map(body, mesh=mesh, in_specs=in_specs, out_specs=out_specs, check_vma=False)
```

```python
import jax
import jax.numpy as jnp
import numpy as np
from jax import lax
from jax.sharding import PartitionSpec as P

SPAN = 128


def block_step(state, inputs):
    query, key_blk, value_blk, decay = inputs
    cum = jnp.cumsum(decay, axis=1)
    size = decay.shape[1]
    rows = lax.broadcasted_iota(jnp.int32, (size, size), 0)
    cols = lax.broadcasted_iota(jnp.int32, (size, size), 1)
    lower = (cols <= rows)[None]
    scores = jnp.einsum("hte,hse->hts", query, key_blk, preferred_element_type=jnp.float32)
    diffs = jnp.where(lower, cum[:, :, None] - cum[:, None, :], 0.0)
    block_weights = (jnp.where(lower, jnp.exp(diffs), 0.0) * scores).astype(jnp.bfloat16)
    intra = jnp.einsum("hts,hse->hte", block_weights, value_blk, preferred_element_type=jnp.float32)
    inter = jnp.exp(cum)[:, :, None] * jnp.einsum(
        "hte,hef->htf", query.astype(jnp.float32), state, precision=lax.Precision.HIGHEST
    )
    total = cum[:, -1]
    scaled_keys = key_blk.astype(jnp.float32) * jnp.exp(total[:, None] - cum)[:, :, None]
    update = jnp.einsum(
        "hse,hsf->hef", scaled_keys, value_blk.astype(jnp.float32), precision=lax.Precision.HIGHEST
    )
    new_state = jnp.exp(total)[:, None, None] * state + update
    return (new_state, intra + inter)


def pack(log_total, memory):
    heads, rows, cols = memory.shape
    extra = jnp.broadcast_to(log_total[:, None, None], (heads, 8, cols))
    return jnp.concatenate([memory, extra], axis=1)


def join(earlier, later):
    rows = earlier.shape[1] - 8
    row = lax.broadcasted_iota(jnp.int32, earlier.shape, 1)
    scale = jnp.where(row < rows, jnp.exp(later[:, rows:rows + 1, :]), 1.0)
    return scale * earlier + later


def member(position, spots):
    bits = 0
    for spot in spots:
        bits |= 1 << spot
    return ((jnp.int32(bits) >> position) & 1) == 1


def line_rounds(width):
    levels = width.bit_length() - 1
    rounds = []

    def both(pairs):
        fwd = [(s, d, True, True) for s, d in pairs]
        bwd = [(width - 1 - s, width - 1 - d, False, False) for s, d in pairs]
        return fwd + bwd

    for k in range(levels - 1):
        step = 1 << k
        rounds.append(both([(p - step, p) for p in range(2 * step - 1, width, 2 * step)]))
    if width >= 2:
        close = [(0, width - 1, False, True), (width - 1, 0, True, False)]
        if levels >= 2:
            step = width // 4
            close += both([(width // 2 - 1, 3 * step - 1)])
        rounds.append(close)
    for k in range(levels - 3, -1, -1):
        step = 1 << k
        rounds.append(both([(p - step, p) for p in range(3 * step - 1, width, 2 * step)]))
    return rounds


def exclusive_scan(parts, axis, lines, width):
    pos = lax.axis_index(axis) % width
    held = list(parts)
    before = [jnp.zeros_like(p) for p in parts]
    after = list(parts)
    if len(parts) > 1:
        held, before, after = lax.optimization_barrier((held, before, after))
    for entries in line_rounds(width):
        assert len({e[0] for e in entries}) == len(entries) and len({e[1] for e in entries}) == len(entries)
        full = [(l * width + e[0], l * width + e[1]) for l in range(lines) for e in entries]
        sends_held = member(pos, [e[0] for e in entries if e[2]])
        into_ahead = member(pos, [e[1] for e in entries if e[3]])
        into_behind = member(pos, [e[1] for e in entries if not e[3]])
        got = [lax.ppermute(jnp.where(sends_held, h, a), axis, full) for h, a in zip(held, after)]
        for i, g in enumerate(got):
            ahead = jnp.where(into_ahead, g, 0.0)
            behind = jnp.where(into_behind, g, 0.0)
            held[i] = join(ahead, held[i])
            before[i] = join(ahead, before[i])
            after[i] = join(after[i], behind)
        if len(parts) > 1:
            held, before, after = lax.optimization_barrier((held, before, after))
    if lines == 1:
        return before
    total = [join(b, a) for b, a in zip(before, after)]
    earlier = [None] * len(parts)
    for shift in range(lines - 1, 0, -1):
        pairs = [((l - shift) * width + p, l * width + p) for l in range(shift, lines) for p in range(width)]
        got = [lax.ppermute(t, axis, pairs) for t in total]
        earlier = [g if e is None else join(e, g) for e, g in zip(earlier, got)]
    return [join(e, b) for e, b in zip(earlier, before)]


def scatter_heads(partial, axis, n):
    rows, total_cols = partial.shape
    width = total_cols // n
    place = lax.axis_index(axis)
    if n % 2 == 0 and n > 2:
        chips = n // 2
        core = place % 2
        chip = place // 2

        def block(index):
            return lax.dynamic_slice_in_dim(partial, index * width, width, 1)

        keep = jnp.stack([block(2 * y + core) for y in range(chips)])
        away = jnp.stack([block(2 * y + 1 - core) for y in range(chips)])
        pairs = [(h, h ^ 1) for h in range(n)]
        mine = keep + lax.ppermute(away, axis, pairs)
        out = lax.dynamic_index_in_dim(mine, chip, 0, False)
        for shift in range(1, chips):
            send = lax.dynamic_index_in_dim(mine, (chip + shift) % chips, 0, False)
            pairs = [(2 * y + c, 2 * ((y + shift) % chips) + c) for y in range(chips) for c in range(2)]
            out = out + lax.ppermute(send, axis, pairs)
        return out
    whole = lax.psum(partial, axis)
    return lax.dynamic_slice_in_dim(whole, place * width, width, 1)


def shards(queries, keys, values, log_decay, norm_gain, out_weight, steer_ids, steer_table, seq_n, seq_width, head_n):
    tok_rows, features = queries.shape
    heads_here = log_decay.shape[1]
    head_size = features // heads_here
    count = tok_rows // SPAN

    def split(array):
        return array.reshape(count, SPAN, heads_here, head_size).transpose(0, 2, 1, 3)

    decays = log_decay.reshape(count, SPAN, heads_here).transpose(0, 2, 1)
    start = jnp.zeros((heads_here, head_size, head_size), jnp.float32)
    local_memory, blocks = lax.scan(
        block_step, start, (split(queries), split(keys), split(values), decays)
    )
    device_log = jnp.sum(log_decay, axis=0)
    lines, width = seq_n // seq_width, seq_width
    packed = pack(device_log, local_memory)
    streams = 2 if heads_here % 2 == 0 else 1
    passed = jnp.concatenate(
        exclusive_scan(jnp.split(packed, streams, axis=0), "seq", lines, width), axis=0
    )
    earlier_memory = passed[:, :head_size, :]
    running = jnp.cumsum(log_decay, axis=0)
    query_heads = queries.reshape(tok_rows, heads_here, head_size).astype(jnp.float32)
    carried = jnp.exp(running)[:, :, None] * jnp.einsum(
        "the,hef->thf", query_heads, earlier_memory, precision=lax.Precision.HIGHEST
    )
    attended = blocks.transpose(0, 2, 1, 3).reshape(tok_rows, heads_here, head_size) + carried
    mean_sq = jnp.mean(attended * attended, axis=-1, keepdims=True)
    normed = (attended * lax.rsqrt(mean_sq + 1e-06)).reshape(tok_rows, features) * norm_gain
    normed = normed.astype(jnp.bfloat16)
    partial_term = lax.optimization_barrier(jnp.dot(normed, out_weight, preferred_element_type=jnp.float32))
    onehot = (
        steer_ids[:, None] == jnp.arange(steer_table.shape[0], dtype=jnp.int32)[None, :]
    ).astype(jnp.bfloat16)
    steering = jnp.dot(onehot, steer_table, preferred_element_type=jnp.float32)
    summed = scatter_heads(partial_term, "head", head_n)
    return (summed + steering).astype(jnp.bfloat16)


def line_width(mesh):
    devices = np.moveaxis(mesh.devices, mesh.axis_names.index("seq"), 0)
    order = devices.reshape(devices.shape[0], -1)[:, 0]
    n = len(order)
    firsts = [tuple(getattr(d, "coords", (0,)))[0] for d in order]
    width = 1
    while width < n and firsts[width] == firsts[0]:
        width += 1
    if n % width or width & (width - 1):
        return n
    return width


def solution(mesh):
    in_specs = (
        P("seq", "head"),
        P("seq", "head"),
        P("seq", "head"),
        P("seq", "head"),
        P("head"),
        P("head", None),
        P("seq"),
        P(None, "head"),
    )
    out_specs = P("seq", "head")
    seq_n = mesh.shape["seq"]
    head_n = mesh.shape["head"]
    seq_width = line_width(mesh)

    def body(*args):
        return shards(*args, seq_n=seq_n, seq_width=seq_width, head_n=head_n)

    return jax.shard_map(body, mesh=mesh, in_specs=in_specs, out_specs=out_specs, check_vma=False)
```

```python
import jax
import jax.numpy as jnp
import numpy as np
from jax import lax
from jax.sharding import PartitionSpec as P

SPAN = 128


def block_step(state, inputs):
    query, key_blk, value_blk, decay = inputs
    cum = jnp.cumsum(decay, axis=1)
    size = decay.shape[1]
    rows = lax.broadcasted_iota(jnp.int32, (size, size), 0)
    cols = lax.broadcasted_iota(jnp.int32, (size, size), 1)
    lower = (cols <= rows)[None]
    scores = jnp.einsum("hte,hse->hts", query, key_blk, preferred_element_type=jnp.float32)
    diffs = jnp.where(lower, cum[:, :, None] - cum[:, None, :], 0.0)
    block_weights = (jnp.where(lower, jnp.exp(diffs), 0.0) * scores).astype(jnp.bfloat16)
    intra = jnp.einsum("hts,hse->hte", block_weights, value_blk, preferred_element_type=jnp.float32)
    inter = jnp.exp(cum)[:, :, None] * jnp.einsum(
        "hte,hef->htf", query.astype(jnp.float32), state, precision=lax.Precision.HIGHEST
    )
    total = cum[:, -1]
    scaled_keys = key_blk.astype(jnp.float32) * jnp.exp(total[:, None] - cum)[:, :, None]
    update = jnp.einsum(
        "hse,hsf->hef", scaled_keys, value_blk.astype(jnp.float32), precision=lax.Precision.HIGHEST
    )
    new_state = jnp.exp(total)[:, None, None] * state + update
    return (new_state, intra + inter)


def pack(log_total, memory):
    heads, rows, cols = memory.shape
    extra = jnp.broadcast_to(log_total[:, None, None], (heads, 8, cols))
    return jnp.concatenate([memory, extra], axis=1)


def join(earlier, later):
    rows = earlier.shape[1] - 8
    row = lax.broadcasted_iota(jnp.int32, earlier.shape, 1)
    scale = jnp.where(row < rows, jnp.exp(later[:, rows:rows + 1, :]), 1.0)
    return scale * earlier + later


def member(position, spots):
    bits = 0
    for spot in spots:
        bits |= 1 << spot
    return ((jnp.int32(bits) >> position) & 1) == 1


def line_rounds(width):
    levels = width.bit_length() - 1
    rounds = []

    def both(pairs):
        fwd = [(s, d, True, True) for s, d in pairs]
        bwd = [(width - 1 - s, width - 1 - d, False, False) for s, d in pairs]
        return fwd + bwd

    for k in range(levels - 1):
        step = 1 << k
        rounds.append(both([(p - step, p) for p in range(2 * step - 1, width, 2 * step)]))
    if width >= 2:
        close = [(0, width - 1, False, True), (width - 1, 0, True, False)]
        if levels >= 2:
            step = width // 4
            close += both([(width // 2 - 1, 3 * step - 1)])
        rounds.append(close)
    for k in range(levels - 3, -1, -1):
        step = 1 << k
        rounds.append(both([(p - step, p) for p in range(3 * step - 1, width, 2 * step)]))
    return rounds


def exclusive_scan(part, axis, lines, width):
    pos = lax.axis_index(axis) % width
    held = part
    before = jnp.zeros_like(part)
    after = part
    for entries in line_rounds(width):
        assert len({e[0] for e in entries}) == len(entries) and len({e[1] for e in entries}) == len(entries)
        send = jnp.where(member(pos, [e[0] for e in entries if e[2]]), held, after)
        full = [(l * width + e[0], l * width + e[1]) for l in range(lines) for e in entries]
        got = lax.ppermute(send, axis, full)
        ahead = jnp.where(member(pos, [e[1] for e in entries if e[3]]), got, 0.0)
        behind = jnp.where(member(pos, [e[1] for e in entries if not e[3]]), got, 0.0)
        held = join(ahead, held)
        before = join(ahead, before)
        after = join(after, behind)
    total = join(before, after)
    if lines == 1:
        return before
    earlier = None
    for shift in range(lines - 1, 0, -1):
        pairs = [((l - shift) * width + p, l * width + p) for l in range(shift, lines) for p in range(width)]
        got = lax.ppermute(total, axis, pairs)
        earlier = got if earlier is None else join(earlier, got)
    return join(earlier, before)


def scatter_heads(partial, axis, n):
    rows, total_cols = partial.shape
    width = total_cols // n
    place = lax.axis_index(axis)
    if n % 2 == 0 and n > 2:
        chips = n // 2
        core = place % 2
        chip = place // 2

        def block(index):
            return lax.dynamic_slice_in_dim(partial, index * width, width, 1)

        if chips == 4:
            def at(shift, parity):
                return block(2 * ((chip + shift) % chips) + parity)

            keep = jnp.stack([at(d, core) for d in (0, 1, 3)])
            away = jnp.stack([at(d, 1 - core) for d in (0, 1, 3)])
            mine = keep + lax.ppermute(away, axis, [(h, h ^ 1) for h in range(n)])
            ring = [(y, c) for y in range(chips) for c in range(2)]
            lower = [(2 * y + c, 2 * ((y - 1) % chips) + c) for y, c in ring]
            upper = [(2 * y + c, 2 * ((y + 1) % chips) + c) for y, c in ring]
            across = [(2 * y + c, 2 * ((y + 1) % chips) + 1 - c) for y, c in ring]
            up = mine[1] + lax.ppermute(at(2, 1 - core), axis, across)
            down = mine[2] + lax.ppermute(at(2, core), axis, lower)
            return mine[0] + lax.ppermute(up, axis, upper) + lax.ppermute(down, axis, lower)

        keep = jnp.stack([block(2 * y + core) for y in range(chips)])
        away = jnp.stack([block(2 * y + 1 - core) for y in range(chips)])
        pairs = [(h, h ^ 1) for h in range(n)]
        mine = keep + lax.ppermute(away, axis, pairs)
        out = lax.dynamic_index_in_dim(mine, chip, 0, False)
        for shift in range(1, chips):
            send = lax.dynamic_index_in_dim(mine, (chip + shift) % chips, 0, False)
            pairs = [(2 * y + c, 2 * ((y + shift) % chips) + c) for y in range(chips) for c in range(2)]
            out = out + lax.ppermute(send, axis, pairs)
        return out
    whole = lax.psum(partial, axis)
    return lax.dynamic_slice_in_dim(whole, place * width, width, 1)


def shards(queries, keys, values, log_decay, norm_gain, out_weight, steer_ids, steer_table, seq_n, seq_width, head_n):
    tok_rows, features = queries.shape
    heads_here = log_decay.shape[1]
    head_size = features // heads_here
    count = tok_rows // SPAN

    def split(array):
        return array.reshape(count, SPAN, heads_here, head_size).transpose(0, 2, 1, 3)

    decays = log_decay.reshape(count, SPAN, heads_here).transpose(0, 2, 1)
    start = jnp.zeros((heads_here, head_size, head_size), jnp.float32)
    local_memory, blocks = lax.scan(
        block_step, start, (split(queries), split(keys), split(values), decays)
    )
    device_log = jnp.sum(log_decay, axis=0)
    lines, width = seq_n // seq_width, seq_width
    passed = exclusive_scan(pack(device_log, local_memory), "seq", lines, width)
    earlier_memory = passed[:, :head_size, :]
    running = jnp.cumsum(log_decay, axis=0)
    query_heads = queries.reshape(tok_rows, heads_here, head_size).astype(jnp.float32)
    carried = jnp.exp(running)[:, :, None] * jnp.einsum(
        "the,hef->thf", query_heads, earlier_memory, precision=lax.Precision.HIGHEST
    )
    attended = blocks.transpose(0, 2, 1, 3).reshape(tok_rows, heads_here, head_size) + carried
    mean_sq = jnp.mean(attended * attended, axis=-1, keepdims=True)
    normed = (attended * lax.rsqrt(mean_sq + 1e-06)).reshape(tok_rows, features) * norm_gain
    normed = normed.astype(jnp.bfloat16)
    partial_term = lax.optimization_barrier(jnp.dot(normed, out_weight, preferred_element_type=jnp.float32))
    onehot = (
        steer_ids[:, None] == jnp.arange(steer_table.shape[0], dtype=jnp.int32)[None, :]
    ).astype(jnp.bfloat16)
    steering = jnp.dot(onehot, steer_table, preferred_element_type=jnp.float32)
    summed = scatter_heads(partial_term, "head", head_n)
    return (summed + steering).astype(jnp.bfloat16)


def line_width(mesh):
    devices = np.moveaxis(mesh.devices, mesh.axis_names.index("seq"), 0)
    order = devices.reshape(devices.shape[0], -1)[:, 0]
    n = len(order)
    firsts = [tuple(getattr(d, "coords", (0,)))[0] for d in order]
    width = 1
    while width < n and firsts[width] == firsts[0]:
        width += 1
    if n % width or width & (width - 1):
        return n
    return width


def solution(mesh):
    in_specs = (
        P("seq", "head"),
        P("seq", "head"),
        P("seq", "head"),
        P("seq", "head"),
        P("head"),
        P("head", None),
        P("seq"),
        P(None, "head"),
    )
    out_specs = P("seq", "head")
    seq_n = mesh.shape["seq"]
    head_n = mesh.shape["head"]
    seq_width = line_width(mesh)

    def body(*args):
        return shards(*args, seq_n=seq_n, seq_width=seq_width, head_n=head_n)

    return jax.shard_map(body, mesh=mesh, in_specs=in_specs, out_specs=out_specs, check_vma=False)
```

```python
import jax
import jax.numpy as jnp
import numpy as np
from jax import lax
from jax.sharding import PartitionSpec as P

SPAN = 128


def block_step(state, inputs):
    query, key_blk, value_blk, decay = inputs
    cum = jnp.cumsum(decay, axis=1)
    size = decay.shape[1]
    rows = lax.broadcasted_iota(jnp.int32, (size, size), 0)
    cols = lax.broadcasted_iota(jnp.int32, (size, size), 1)
    lower = (cols <= rows)[None]
    scores = jnp.einsum("hte,hse->hts", query, key_blk, preferred_element_type=jnp.float32)
    diffs = jnp.where(lower, cum[:, :, None] - cum[:, None, :], 0.0)
    block_weights = (jnp.where(lower, jnp.exp(diffs), 0.0) * scores).astype(jnp.bfloat16)
    intra = jnp.einsum("hts,hse->hte", block_weights, value_blk, preferred_element_type=jnp.float32)
    inter = jnp.exp(cum)[:, :, None] * jnp.einsum(
        "hte,hef->htf", query.astype(jnp.float32), state, precision=lax.Precision.HIGHEST
    )
    total = cum[:, -1]
    scaled_keys = key_blk.astype(jnp.float32) * jnp.exp(total[:, None] - cum)[:, :, None]
    update = jnp.einsum(
        "hse,hsf->hef", scaled_keys, value_blk.astype(jnp.float32), precision=lax.Precision.HIGHEST
    )
    new_state = jnp.exp(total)[:, None, None] * state + update
    return (new_state, intra + inter)


def pack(log_total, memory):
    heads, rows, cols = memory.shape
    extra = jnp.broadcast_to(log_total[:, None, None], (heads, 8, cols))
    return jnp.concatenate([memory, extra], axis=1)


def join(earlier, later):
    rows = earlier.shape[1] - 8
    row = lax.broadcasted_iota(jnp.int32, earlier.shape, 1)
    scale = jnp.where(row < rows, jnp.exp(later[:, rows:rows + 1, :]), 1.0)
    return scale * earlier + later


def member(position, spots):
    bits = 0
    for spot in spots:
        bits |= 1 << spot
    return ((jnp.int32(bits) >> position) & 1) == 1


def line_rounds(width):
    levels = width.bit_length() - 1
    rounds = []

    def both(pairs):
        fwd = [(s, d, True, True) for s, d in pairs]
        bwd = [(width - 1 - s, width - 1 - d, False, False) for s, d in pairs]
        return fwd + bwd

    for k in range(levels - 1):
        step = 1 << k
        rounds.append(both([(p - step, p) for p in range(2 * step - 1, width, 2 * step)]))
    if width >= 2:
        close = [(0, width - 1, False, True), (width - 1, 0, True, False)]
        if levels >= 2:
            step = width // 4
            close += both([(width // 2 - 1, 3 * step - 1)])
        rounds.append(close)
    for k in range(levels - 3, -1, -1):
        step = 1 << k
        rounds.append(both([(p - step, p) for p in range(3 * step - 1, width, 2 * step)]))
    return rounds


def exclusive_scan(part, axis, lines, width):
    pos = lax.axis_index(axis) % width
    held = part
    before = jnp.zeros_like(part)
    after = part
    for entries in line_rounds(width):
        assert len({e[0] for e in entries}) == len(entries) and len({e[1] for e in entries}) == len(entries)
        send = jnp.where(member(pos, [e[0] for e in entries if e[2]]), held, after)
        full = [(l * width + e[0], l * width + e[1]) for l in range(lines) for e in entries]
        got = lax.ppermute(send, axis, full)
        ahead = jnp.where(member(pos, [e[1] for e in entries if e[3]]), got, 0.0)
        behind = jnp.where(member(pos, [e[1] for e in entries if not e[3]]), got, 0.0)
        held = join(ahead, held)
        before = join(ahead, before)
        after = join(after, behind)
    total = join(before, after)
    if lines == 1:
        return before
    earlier = None
    for shift in range(lines - 1, 0, -1):
        pairs = [((l - shift) * width + p, l * width + p) for l in range(shift, lines) for p in range(width)]
        got = lax.ppermute(total, axis, pairs)
        earlier = got if earlier is None else join(earlier, got)
    return join(earlier, before)


def scatter_heads(block, n, width, axis):
    place = lax.axis_index(axis)
    if n % 2 == 0 and n > 2:
        chips = n // 2
        core = place % 2
        chip = place // 2
        away = jnp.stack([block(2 * y + 1 - core) for y in range(chips)])
        moved = lax.ppermute(away, axis, [(h, h ^ 1) for h in range(n)])
        keep = jnp.stack([block(2 * y + core) for y in range(chips)])
        mine = keep + moved
        out = lax.dynamic_index_in_dim(mine, chip, 0, False)
        shifts = sorted(range(1, chips), key=lambda s: -min(s, chips - s))
        for shift in shifts:
            send = lax.dynamic_index_in_dim(mine, (chip + shift) % chips, 0, False)
            pairs = [(2 * y + c, 2 * ((y + shift) % chips) + c) for y in range(chips) for c in range(2)]
            out = out + lax.ppermute(send, axis, pairs)
        return out
    whole = jnp.concatenate([block(i) for i in range(n)], axis=1)
    whole = lax.psum(whole, axis)
    return lax.dynamic_slice_in_dim(whole, place * width, width, 1)


def shards(queries, keys, values, log_decay, norm_gain, out_weight, steer_ids, steer_table, seq_n, seq_width, head_n):
    tok_rows, features = queries.shape
    heads_here = log_decay.shape[1]
    head_size = features // heads_here
    count = tok_rows // SPAN

    def split(array):
        return array.reshape(count, SPAN, heads_here, head_size).transpose(0, 2, 1, 3)

    decays = log_decay.reshape(count, SPAN, heads_here).transpose(0, 2, 1)
    start = jnp.zeros((heads_here, head_size, head_size), jnp.float32)
    local_memory, blocks = lax.scan(
        block_step, start, (split(queries), split(keys), split(values), decays)
    )
    device_log = jnp.sum(log_decay, axis=0)
    lines, width = seq_n // seq_width, seq_width
    passed = exclusive_scan(pack(device_log, local_memory), "seq", lines, width)
    earlier_memory = passed[:, :head_size, :]
    running = jnp.cumsum(log_decay, axis=0)
    query_heads = queries.reshape(tok_rows, heads_here, head_size).astype(jnp.float32)
    carried = jnp.exp(running)[:, :, None] * jnp.einsum(
        "the,hef->thf", query_heads, earlier_memory, precision=lax.Precision.HIGHEST
    )
    attended = blocks.transpose(0, 2, 1, 3).reshape(tok_rows, heads_here, head_size) + carried
    mean_sq = jnp.mean(attended * attended, axis=-1, keepdims=True)
    normed = (attended * lax.rsqrt(mean_sq + 1e-06)).reshape(tok_rows, features) * norm_gain
    normed = normed.astype(jnp.bfloat16)
    width = out_weight.shape[1] // head_n

    def block(index):
        cols = lax.dynamic_slice_in_dim(out_weight, index * width, width, 1)
        return jnp.dot(normed, cols, preferred_element_type=jnp.float32)

    onehot = (
        steer_ids[:, None] == jnp.arange(steer_table.shape[0], dtype=jnp.int32)[None, :]
    ).astype(jnp.bfloat16)
    steering = jnp.dot(onehot, steer_table, preferred_element_type=jnp.float32)
    summed = scatter_heads(block, head_n, width, "head")
    return (summed + steering).astype(jnp.bfloat16)


def line_width(mesh):
    devices = np.moveaxis(mesh.devices, mesh.axis_names.index("seq"), 0)
    order = devices.reshape(devices.shape[0], -1)[:, 0]
    n = len(order)
    firsts = [tuple(getattr(d, "coords", (0,)))[0] for d in order]
    width = 1
    while width < n and firsts[width] == firsts[0]:
        width += 1
    if n % width or width & (width - 1):
        return n
    return width


def solution(mesh):
    in_specs = (
        P("seq", "head"),
        P("seq", "head"),
        P("seq", "head"),
        P("seq", "head"),
        P("head"),
        P("head", None),
        P("seq"),
        P(None, "head"),
    )
    out_specs = P("seq", "head")
    seq_n = mesh.shape["seq"]
    head_n = mesh.shape["head"]
    seq_width = line_width(mesh)

    def body(*args):
        return shards(*args, seq_n=seq_n, seq_width=seq_width, head_n=head_n)

    return jax.shard_map(body, mesh=mesh, in_specs=in_specs, out_specs=out_specs, check_vma=False)
```

```python
import jax
import jax.numpy as jnp
import numpy as np
from jax import lax
from jax.sharding import PartitionSpec as P

SPAN = 128


def block_step(state, inputs):
    query, key_blk, value_blk, decay = inputs
    cum = jnp.cumsum(decay, axis=1)
    size = decay.shape[1]
    rows = lax.broadcasted_iota(jnp.int32, (size, size), 0)
    cols = lax.broadcasted_iota(jnp.int32, (size, size), 1)
    lower = (cols <= rows)[None]
    scores = jnp.einsum("hte,hse->hts", query, key_blk, preferred_element_type=jnp.float32)
    diffs = jnp.where(lower, cum[:, :, None] - cum[:, None, :], 0.0)
    block_weights = (jnp.where(lower, jnp.exp(diffs), 0.0) * scores).astype(jnp.bfloat16)
    intra = jnp.einsum("hts,hse->hte", block_weights, value_blk, preferred_element_type=jnp.float32)
    inter = jnp.exp(cum)[:, :, None] * jnp.einsum(
        "hte,hef->htf", query.astype(jnp.float32), state, precision=lax.Precision.HIGHEST
    )
    total = cum[:, -1]
    scaled_keys = key_blk.astype(jnp.float32) * jnp.exp(total[:, None] - cum)[:, :, None]
    update = jnp.einsum(
        "hse,hsf->hef", scaled_keys, value_blk.astype(jnp.float32), precision=lax.Precision.HIGHEST
    )
    new_state = jnp.exp(total)[:, None, None] * state + update
    return (new_state, intra + inter)


def pack(log_total, memory):
    heads, rows, cols = memory.shape
    extra = jnp.broadcast_to(log_total[:, None, None], (heads, 8, cols))
    return jnp.concatenate([memory, extra], axis=1)


def join(earlier, later):
    rows = earlier.shape[1] - 8
    row = lax.broadcasted_iota(jnp.int32, earlier.shape, 1)
    scale = jnp.where(row < rows, jnp.exp(later[:, rows:rows + 1, :]), 1.0)
    return scale * earlier + later


def member(position, spots):
    bits = 0
    for spot in spots:
        bits |= 1 << spot
    return ((jnp.int32(bits) >> position) & 1) == 1


def line_rounds(width):
    levels = width.bit_length() - 1
    rounds = []

    def both(pairs):
        fwd = [(s, d, True, True) for s, d in pairs]
        bwd = [(width - 1 - s, width - 1 - d, False, False) for s, d in pairs]
        return fwd + bwd

    for k in range(levels - 1):
        step = 1 << k
        rounds.append(both([(p - step, p) for p in range(2 * step - 1, width, 2 * step)]))
    if width >= 2:
        close = [(0, width - 1, False, True), (width - 1, 0, True, False)]
        if levels >= 2:
            step = width // 4
            close += both([(width // 2 - 1, 3 * step - 1)])
        rounds.append(close)
    for k in range(levels - 3, -1, -1):
        step = 1 << k
        rounds.append(both([(p - step, p) for p in range(3 * step - 1, width, 2 * step)]))
    return rounds


def exclusive_scan(part, axis, lines, width):
    pos = lax.axis_index(axis) % width
    held = part
    before = jnp.zeros_like(part)
    after = part
    for entries in line_rounds(width):
        assert len({e[0] for e in entries}) == len(entries) and len({e[1] for e in entries}) == len(entries)
        send = jnp.where(member(pos, [e[0] for e in entries if e[2]]), held, after)
        full = [(l * width + e[0], l * width + e[1]) for l in range(lines) for e in entries]
        got = lax.ppermute(send, axis, full)
        ahead = jnp.where(member(pos, [e[1] for e in entries if e[3]]), got, 0.0)
        behind = jnp.where(member(pos, [e[1] for e in entries if not e[3]]), got, 0.0)
        held = join(ahead, held)
        before = join(ahead, before)
        after = join(after, behind)
    total = join(before, after)
    if lines == 1:
        return before
    earlier = None
    for shift in range(lines - 1, 0, -1):
        pairs = [((l - shift) * width + p, l * width + p) for l in range(shift, lines) for p in range(width)]
        got = lax.ppermute(total, axis, pairs)
        earlier = got if earlier is None else join(earlier, got)
    return join(earlier, before)


def scatter_heads(partial, axis, n):
    rows, total_cols = partial.shape
    width = total_cols // n
    place = lax.axis_index(axis)
    if n % 2 == 0 and n > 2:
        chips = n // 2
        core = place % 2
        chip = place // 2

        def block(index):
            return lax.dynamic_slice_in_dim(partial, index * width, width, 1)

        keep = jnp.stack([block(2 * y + core) for y in range(chips)])
        away = jnp.stack([block(2 * y + 1 - core) for y in range(chips)])
        pairs = [(h, h ^ 1) for h in range(n)]
        mine = keep + lax.ppermute(away, axis, pairs)
        out = lax.dynamic_index_in_dim(mine, chip, 0, False)
        for shift in range(1, chips):
            send = lax.dynamic_index_in_dim(mine, (chip + shift) % chips, 0, False)
            pairs = [(2 * y + c, 2 * ((y + shift) % chips) + c) for y in range(chips) for c in range(2)]
            out = out + lax.ppermute(send, axis, pairs)
        return out
    whole = lax.psum(partial, axis)
    return lax.dynamic_slice_in_dim(whole, place * width, width, 1)


def shards(queries, keys, values, log_decay, norm_gain, out_weight, steer_ids, steer_table, seq_n, seq_width, head_n):
    tok_rows, features = queries.shape
    heads_here = log_decay.shape[1]
    head_size = features // heads_here
    count = tok_rows // SPAN

    def split(array):
        return array.reshape(count, SPAN, heads_here, head_size).transpose(0, 2, 1, 3)

    decays = log_decay.reshape(count, SPAN, heads_here).transpose(0, 2, 1)
    start = jnp.zeros((heads_here, head_size, head_size), jnp.float32)
    def step_with_total(state, inputs):
        new_state, out = block_step(state, inputs)
        return new_state, (out, jnp.cumsum(inputs[3], axis=1)[:, -1])

    local_memory, (blocks, block_logs) = lax.scan(
        step_with_total, start, (split(queries), split(keys), split(values), decays)
    )
    device_log = jnp.sum(block_logs, axis=0)
    lines, width = seq_n // seq_width, seq_width
    passed = exclusive_scan(pack(device_log, local_memory), "seq", lines, width)
    earlier_memory = passed[:, :head_size, :]
    running = jnp.cumsum(log_decay, axis=0)
    query_heads = queries.reshape(tok_rows, heads_here, head_size).astype(jnp.float32)
    carried = jnp.exp(running)[:, :, None] * jnp.einsum(
        "the,hef->thf", query_heads, earlier_memory, precision=lax.Precision.HIGHEST
    )
    attended = blocks.transpose(0, 2, 1, 3).reshape(tok_rows, heads_here, head_size) + carried
    mean_sq = jnp.mean(attended * attended, axis=-1, keepdims=True)
    normed = (attended * lax.rsqrt(mean_sq + 1e-06)).reshape(tok_rows, features) * norm_gain
    normed = normed.astype(jnp.bfloat16)
    partial_term = lax.optimization_barrier(jnp.dot(normed, out_weight, preferred_element_type=jnp.float32))
    onehot = (
        steer_ids[:, None] == jnp.arange(steer_table.shape[0], dtype=jnp.int32)[None, :]
    ).astype(jnp.bfloat16)
    steering = jnp.dot(onehot, steer_table, preferred_element_type=jnp.float32)
    summed = scatter_heads(partial_term, "head", head_n)
    return (summed + steering).astype(jnp.bfloat16)


def line_width(mesh):
    devices = np.moveaxis(mesh.devices, mesh.axis_names.index("seq"), 0)
    order = devices.reshape(devices.shape[0], -1)[:, 0]
    n = len(order)
    firsts = [tuple(getattr(d, "coords", (0,)))[0] for d in order]
    width = 1
    while width < n and firsts[width] == firsts[0]:
        width += 1
    if n % width or width & (width - 1):
        return n
    return width


def solution(mesh):
    in_specs = (
        P("seq", "head"),
        P("seq", "head"),
        P("seq", "head"),
        P("seq", "head"),
        P("head"),
        P("head", None),
        P("seq"),
        P(None, "head"),
    )
    out_specs = P("seq", "head")
    seq_n = mesh.shape["seq"]
    head_n = mesh.shape["head"]
    seq_width = line_width(mesh)

    def body(*args):
        return shards(*args, seq_n=seq_n, seq_width=seq_width, head_n=head_n)

    return jax.shard_map(body, mesh=mesh, in_specs=in_specs, out_specs=out_specs, check_vma=False)
```

```python
import jax
import jax.numpy as jnp
import numpy as np
from jax import lax
from jax.sharding import PartitionSpec as P

SPAN = 128


def block_step(state, inputs):
    query, key_blk, value_blk, decay = inputs
    cum = jnp.cumsum(decay, axis=1)
    size = decay.shape[1]
    rows = lax.broadcasted_iota(jnp.int32, (size, size), 0)
    cols = lax.broadcasted_iota(jnp.int32, (size, size), 1)
    lower = (cols <= rows)[None]
    scores = jnp.einsum("hte,hse->hts", query, key_blk, preferred_element_type=jnp.float32)
    diffs = jnp.where(lower, cum[:, :, None] - cum[:, None, :], 0.0)
    block_weights = (jnp.where(lower, jnp.exp(diffs), 0.0) * scores).astype(jnp.bfloat16)
    intra = jnp.einsum("hts,hse->hte", block_weights, value_blk, preferred_element_type=jnp.float32)
    inter = jnp.exp(cum)[:, :, None] * jnp.einsum(
        "hte,hef->htf", query.astype(jnp.float32), state, precision=lax.Precision.HIGHEST
    )
    total = cum[:, -1]
    scaled_keys = key_blk.astype(jnp.float32) * jnp.exp(total[:, None] - cum)[:, :, None]
    update = jnp.einsum(
        "hse,hsf->hef", scaled_keys, value_blk.astype(jnp.float32), precision=lax.Precision.HIGHEST
    )
    new_state = jnp.exp(total)[:, None, None] * state + update
    return (new_state, intra + inter)


def pack(log_total, memory):
    heads, rows, cols = memory.shape
    extra = jnp.broadcast_to(log_total[:, None], (heads, cols))
    pad = jnp.zeros(((-heads) % 8, cols), memory.dtype)
    return jnp.concatenate([memory.reshape(heads * rows, cols), extra, pad], axis=0)


def unpack(packed, heads, rows):
    return packed[: heads * rows].reshape(heads, rows, -1)


def join(earlier, later, heads, rows):
    size = heads * rows
    scale = jnp.exp(later[size:size + heads])[:, None, :]
    memory = scale * unpack(earlier, heads, rows) + unpack(later, heads, rows)
    logs = earlier[size:] + later[size:]
    return jnp.concatenate([memory.reshape(size, -1), logs], axis=0)


def member(position, spots):
    bits = 0
    for spot in spots:
        bits |= 1 << spot
    return ((jnp.int32(bits) >> position) & 1) == 1


def line_rounds(width):
    levels = width.bit_length() - 1
    rounds = []

    def both(pairs):
        fwd = [(s, d, True, True) for s, d in pairs]
        bwd = [(width - 1 - s, width - 1 - d, False, False) for s, d in pairs]
        return fwd + bwd

    for k in range(levels - 1):
        step = 1 << k
        rounds.append(both([(p - step, p) for p in range(2 * step - 1, width, 2 * step)]))
    if width >= 2:
        close = [(0, width - 1, False, True), (width - 1, 0, True, False)]
        if levels >= 2:
            step = width // 4
            close += both([(width // 2 - 1, 3 * step - 1)])
        rounds.append(close)
    for k in range(levels - 3, -1, -1):
        step = 1 << k
        rounds.append(both([(p - step, p) for p in range(3 * step - 1, width, 2 * step)]))
    return rounds


def exclusive_scan(part, axis, lines, width, heads, rows):
    pos = lax.axis_index(axis) % width
    held = part
    before = jnp.zeros_like(part)
    after = part
    for entries in line_rounds(width):
        assert len({e[0] for e in entries}) == len(entries) and len({e[1] for e in entries}) == len(entries)
        send = jnp.where(member(pos, [e[0] for e in entries if e[2]]), held, after)
        full = [(l * width + e[0], l * width + e[1]) for l in range(lines) for e in entries]
        got = lax.ppermute(send, axis, full)
        ahead = jnp.where(member(pos, [e[1] for e in entries if e[3]]), got, 0.0)
        behind = jnp.where(member(pos, [e[1] for e in entries if not e[3]]), got, 0.0)
        held = join(ahead, held, heads, rows)
        before = join(ahead, before, heads, rows)
        after = join(after, behind, heads, rows)
    total = join(before, after, heads, rows)
    if lines == 1:
        return before
    earlier = None
    for shift in range(lines - 1, 0, -1):
        pairs = [((l - shift) * width + p, l * width + p) for l in range(shift, lines) for p in range(width)]
        got = lax.ppermute(total, axis, pairs)
        earlier = got if earlier is None else join(earlier, got, heads, rows)
    return join(earlier, before, heads, rows)


def scatter_heads(partial, axis, n):
    rows, total_cols = partial.shape
    width = total_cols // n
    place = lax.axis_index(axis)
    if n % 2 == 0 and n > 2:
        chips = n // 2
        core = place % 2
        chip = place // 2

        def block(index):
            return lax.dynamic_slice_in_dim(partial, index * width, width, 1)

        keep = jnp.stack([block(2 * y + core) for y in range(chips)])
        away = jnp.stack([block(2 * y + 1 - core) for y in range(chips)])
        pairs = [(h, h ^ 1) for h in range(n)]
        mine = keep + lax.ppermute(away, axis, pairs)
        out = lax.dynamic_index_in_dim(mine, chip, 0, False)
        for shift in range(1, chips):
            send = lax.dynamic_index_in_dim(mine, (chip + shift) % chips, 0, False)
            pairs = [(2 * y + c, 2 * ((y + shift) % chips) + c) for y in range(chips) for c in range(2)]
            out = out + lax.ppermute(send, axis, pairs)
        return out
    whole = lax.psum(partial, axis)
    return lax.dynamic_slice_in_dim(whole, place * width, width, 1)


def shards(queries, keys, values, log_decay, norm_gain, out_weight, steer_ids, steer_table, seq_n, seq_width, head_n):
    tok_rows, features = queries.shape
    heads_here = log_decay.shape[1]
    head_size = features // heads_here
    count = tok_rows // SPAN

    def split(array):
        return array.reshape(count, SPAN, heads_here, head_size).transpose(0, 2, 1, 3)

    decays = log_decay.reshape(count, SPAN, heads_here).transpose(0, 2, 1)
    start = jnp.zeros((heads_here, head_size, head_size), jnp.float32)
    def step_with_total(state, inputs):
        new_state, out = block_step(state, inputs)
        return new_state, (out, jnp.cumsum(inputs[3], axis=1)[:, -1])

    local_memory, (blocks, block_logs) = lax.scan(
        step_with_total, start, (split(queries), split(keys), split(values), decays)
    )
    device_log = jnp.sum(block_logs, axis=0)
    lines, width = seq_n // seq_width, seq_width
    passed = exclusive_scan(pack(device_log, local_memory), "seq", lines, width, heads_here, head_size)
    earlier_memory = unpack(passed, heads_here, head_size)
    running = jnp.cumsum(log_decay, axis=0)
    query_heads = queries.reshape(tok_rows, heads_here, head_size).astype(jnp.float32)
    carried = jnp.exp(running)[:, :, None] * jnp.einsum(
        "the,hef->thf", query_heads, earlier_memory, precision=lax.Precision.HIGHEST
    )
    attended = blocks.transpose(0, 2, 1, 3).reshape(tok_rows, heads_here, head_size) + carried
    mean_sq = jnp.mean(attended * attended, axis=-1, keepdims=True)
    normed = (attended * lax.rsqrt(mean_sq + 1e-06)).reshape(tok_rows, features) * norm_gain
    normed = normed.astype(jnp.bfloat16)
    partial_term = lax.optimization_barrier(jnp.dot(normed, out_weight, preferred_element_type=jnp.float32))
    onehot = (
        steer_ids[:, None] == jnp.arange(steer_table.shape[0], dtype=jnp.int32)[None, :]
    ).astype(jnp.bfloat16)
    steering = jnp.dot(onehot, steer_table, preferred_element_type=jnp.float32)
    summed = scatter_heads(partial_term, "head", head_n)
    return (summed + steering).astype(jnp.bfloat16)


def line_width(mesh):
    devices = np.moveaxis(mesh.devices, mesh.axis_names.index("seq"), 0)
    order = devices.reshape(devices.shape[0], -1)[:, 0]
    n = len(order)
    firsts = [tuple(getattr(d, "coords", (0,)))[0] for d in order]
    width = 1
    while width < n and firsts[width] == firsts[0]:
        width += 1
    if n % width or width & (width - 1):
        return n
    return width


def solution(mesh):
    in_specs = (
        P("seq", "head"),
        P("seq", "head"),
        P("seq", "head"),
        P("seq", "head"),
        P("head"),
        P("head", None),
        P("seq"),
        P(None, "head"),
    )
    out_specs = P("seq", "head")
    seq_n = mesh.shape["seq"]
    head_n = mesh.shape["head"]
    seq_width = line_width(mesh)

    def body(*args):
        return shards(*args, seq_n=seq_n, seq_width=seq_width, head_n=head_n)

    return jax.shard_map(body, mesh=mesh, in_specs=in_specs, out_specs=out_specs, check_vma=False)
```

```python
import jax
import jax.numpy as jnp
import numpy as np
from jax import lax
from jax.sharding import PartitionSpec as P

SPAN = 128


def block_step(state, inputs):
    query, key_blk, value_blk, decay = inputs
    cum = jnp.cumsum(decay, axis=1)
    size = decay.shape[1]
    rows = lax.broadcasted_iota(jnp.int32, (size, size), 0)
    cols = lax.broadcasted_iota(jnp.int32, (size, size), 1)
    lower = (cols <= rows)[None]
    scores = jnp.einsum("hte,hse->hts", query, key_blk, preferred_element_type=jnp.float32)
    diffs = jnp.where(lower, cum[:, :, None] - cum[:, None, :], 0.0)
    block_weights = (jnp.where(lower, jnp.exp(diffs), 0.0) * scores).astype(jnp.bfloat16)
    intra = jnp.einsum("hts,hse->hte", block_weights, value_blk, preferred_element_type=jnp.float32)
    inter = jnp.exp(cum)[:, :, None] * jnp.einsum(
        "hte,hef->htf", query.astype(jnp.float32), state, precision=lax.Precision.HIGHEST
    )
    total = cum[:, -1]
    scaled_keys = key_blk.astype(jnp.float32) * jnp.exp(total[:, None] - cum)[:, :, None]
    update = jnp.einsum(
        "hse,hsf->hef", scaled_keys, value_blk.astype(jnp.float32), precision=lax.Precision.HIGHEST
    )
    new_state = jnp.exp(total)[:, None, None] * state + update
    return (new_state, intra + inter)


def pack(log_total, memory):
    heads, rows, cols = memory.shape
    extra = jnp.broadcast_to(log_total[:, None], (heads, cols))
    pad = jnp.zeros(((-heads) % 8, cols), memory.dtype)
    return jnp.concatenate([memory.reshape(heads * rows, cols), extra, pad], axis=0)


def unpack(packed, heads, rows):
    return packed[: heads * rows].reshape(heads, rows, -1)


def join(earlier, later, heads, rows):
    size = heads * rows
    scale = jnp.exp(later[size:size + heads])[:, None, :]
    memory = scale * unpack(earlier, heads, rows) + unpack(later, heads, rows)
    logs = earlier[size:] + later[size:]
    return jnp.concatenate([memory.reshape(size, -1), logs], axis=0)


def member(position, spots):
    bits = 0
    for spot in spots:
        bits |= 1 << spot
    return ((jnp.int32(bits) >> position) & 1) == 1


def line_rounds(width):
    levels = width.bit_length() - 1
    rounds = []

    def both(pairs):
        fwd = [(s, d, True, True) for s, d in pairs]
        bwd = [(width - 1 - s, width - 1 - d, False, False) for s, d in pairs]
        return fwd + bwd

    for k in range(levels - 1):
        step = 1 << k
        rounds.append(both([(p - step, p) for p in range(2 * step - 1, width, 2 * step)]))
    if width >= 2:
        close = [(0, width - 1, False, True), (width - 1, 0, True, False)]
        if levels >= 2:
            step = width // 4
            close += both([(width // 2 - 1, 3 * step - 1)])
        rounds.append(close)
    for k in range(levels - 3, -1, -1):
        step = 1 << k
        rounds.append(both([(p - step, p) for p in range(3 * step - 1, width, 2 * step)]))
    return rounds


def exclusive_scan(part, axis, lines, width, heads, rows):
    pos = lax.axis_index(axis) % width
    held = part
    before = jnp.zeros_like(part)
    after = part
    for entries in line_rounds(width):
        assert len({e[0] for e in entries}) == len(entries) and len({e[1] for e in entries}) == len(entries)
        send = jnp.where(member(pos, [e[0] for e in entries if e[2]]), held, after)
        full = [(l * width + e[0], l * width + e[1]) for l in range(lines) for e in entries]
        got = lax.ppermute(send, axis, full)
        ahead = jnp.where(member(pos, [e[1] for e in entries if e[3]]), got, 0.0)
        behind = jnp.where(member(pos, [e[1] for e in entries if not e[3]]), got, 0.0)
        held = join(ahead, held, heads, rows)
        before = join(ahead, before, heads, rows)
        after = join(after, behind, heads, rows)
    total = join(before, after, heads, rows)
    if lines == 1:
        return before
    earlier = None
    for shift in range(lines - 1, 0, -1):
        pairs = [((l - shift) * width + p, l * width + p) for l in range(shift, lines) for p in range(width)]
        got = lax.ppermute(total, axis, pairs)
        earlier = got if earlier is None else join(earlier, got, heads, rows)
    return join(earlier, before, heads, rows)


def scatter_heads(partial, axis, n):
    rows, total_cols = partial.shape
    width = total_cols // n
    place = lax.axis_index(axis)
    if n % 2 == 0 and n > 2:
        chips = n // 2
        core = place % 2
        chip = place // 2

        def block(index):
            return lax.dynamic_slice_in_dim(partial, index * width, width, 1)

        keep = jnp.stack([block(2 * y + core) for y in range(chips)])
        away = jnp.stack([block(2 * y + 1 - core) for y in range(chips)])
        pairs = [(h, h ^ 1) for h in range(n)]
        mine = keep + lax.ppermute(away, axis, pairs)
        out = lax.dynamic_index_in_dim(mine, chip, 0, False)
        for shift in sorted(range(1, chips), key=lambda s: -min(s, chips - s)):
            send = lax.dynamic_index_in_dim(mine, (chip + shift) % chips, 0, False)
            pairs = [(2 * y + c, 2 * ((y + shift) % chips) + c) for y in range(chips) for c in range(2)]
            out = out + lax.ppermute(send, axis, pairs)
        return out
    whole = lax.psum(partial, axis)
    return lax.dynamic_slice_in_dim(whole, place * width, width, 1)


def shards(queries, keys, values, log_decay, norm_gain, out_weight, steer_ids, steer_table, seq_n, seq_width, head_n):
    tok_rows, features = queries.shape
    heads_here = log_decay.shape[1]
    head_size = features // heads_here
    count = tok_rows // SPAN

    def split(array):
        return array.reshape(count, SPAN, heads_here, head_size).transpose(0, 2, 1, 3)

    decays = log_decay.reshape(count, SPAN, heads_here).transpose(0, 2, 1)
    start = jnp.zeros((heads_here, head_size, head_size), jnp.float32)
    def step_with_total(state, inputs):
        new_state, out = block_step(state, inputs)
        return new_state, (out, jnp.cumsum(inputs[3], axis=1)[:, -1])

    local_memory, (blocks, block_logs) = lax.scan(
        step_with_total, start, (split(queries), split(keys), split(values), decays)
    )
    device_log = jnp.sum(block_logs, axis=0)
    lines, width = seq_n // seq_width, seq_width
    passed = exclusive_scan(pack(device_log, local_memory), "seq", lines, width, heads_here, head_size)
    earlier_memory = unpack(passed, heads_here, head_size)
    running = jnp.cumsum(log_decay, axis=0)
    query_heads = queries.reshape(tok_rows, heads_here, head_size).astype(jnp.float32)
    carried = jnp.exp(running)[:, :, None] * jnp.einsum(
        "the,hef->thf", query_heads, earlier_memory, precision=lax.Precision.HIGHEST
    )
    attended = blocks.transpose(0, 2, 1, 3).reshape(tok_rows, heads_here, head_size) + carried
    mean_sq = jnp.mean(attended * attended, axis=-1, keepdims=True)
    normed = (attended * lax.rsqrt(mean_sq + 1e-06)).reshape(tok_rows, features) * norm_gain
    normed = normed.astype(jnp.bfloat16)
    partial_term = lax.optimization_barrier(jnp.dot(normed, out_weight, preferred_element_type=jnp.float32))
    onehot = (
        steer_ids[:, None] == jnp.arange(steer_table.shape[0], dtype=jnp.int32)[None, :]
    ).astype(jnp.bfloat16)
    steering = jnp.dot(onehot, steer_table, preferred_element_type=jnp.float32)
    summed = scatter_heads(partial_term, "head", head_n)
    return (summed + steering).astype(jnp.bfloat16)


def line_width(mesh):
    devices = np.moveaxis(mesh.devices, mesh.axis_names.index("seq"), 0)
    order = devices.reshape(devices.shape[0], -1)[:, 0]
    n = len(order)
    firsts = [tuple(getattr(d, "coords", (0,)))[0] for d in order]
    width = 1
    while width < n and firsts[width] == firsts[0]:
        width += 1
    if n % width or width & (width - 1):
        return n
    return width


def solution(mesh):
    in_specs = (
        P("seq", "head"),
        P("seq", "head"),
        P("seq", "head"),
        P("seq", "head"),
        P("head"),
        P("head", None),
        P("seq"),
        P(None, "head"),
    )
    out_specs = P("seq", "head")
    seq_n = mesh.shape["seq"]
    head_n = mesh.shape["head"]
    seq_width = line_width(mesh)

    def body(*args):
        return shards(*args, seq_n=seq_n, seq_width=seq_width, head_n=head_n)

    return jax.shard_map(body, mesh=mesh, in_specs=in_specs, out_specs=out_specs, check_vma=False)
```

```python
import jax
import jax.numpy as jnp
import numpy as np
from jax import lax
from jax.sharding import PartitionSpec as P

SPAN = 128


def block_step(state, inputs):
    query, key_blk, value_blk, decay = inputs
    cum = jnp.cumsum(decay, axis=1)
    size = decay.shape[1]
    rows = lax.broadcasted_iota(jnp.int32, (size, size), 0)
    cols = lax.broadcasted_iota(jnp.int32, (size, size), 1)
    lower = (cols <= rows)[None]
    scores = jnp.einsum("hte,hse->hts", query, key_blk, preferred_element_type=jnp.float32)
    diffs = jnp.where(lower, cum[:, :, None] - cum[:, None, :], 0.0)
    block_weights = (jnp.where(lower, jnp.exp(diffs), 0.0) * scores).astype(jnp.bfloat16)
    intra = jnp.einsum("hts,hse->hte", block_weights, value_blk, preferred_element_type=jnp.float32)
    inter = jnp.exp(cum)[:, :, None] * jnp.einsum(
        "hte,hef->htf", query.astype(jnp.float32), state, precision=lax.Precision.HIGHEST
    )
    total = cum[:, -1]
    scaled_keys = key_blk.astype(jnp.float32) * jnp.exp(total[:, None] - cum)[:, :, None]
    update = jnp.einsum(
        "hse,hsf->hef", scaled_keys, value_blk.astype(jnp.float32), precision=lax.Precision.HIGHEST
    )
    new_state = jnp.exp(total)[:, None, None] * state + update
    return (new_state, intra + inter)


def pack(log_total, memory):
    heads, rows, cols = memory.shape
    extra = jnp.broadcast_to(log_total[:, None], (heads, cols))
    pad = jnp.zeros(((-heads) % 8, cols), memory.dtype)
    return jnp.concatenate([memory.reshape(heads * rows, cols), extra, pad], axis=0)


def unpack(packed, heads, rows):
    return packed[: heads * rows].reshape(heads, rows, -1)


def join(earlier, later, heads, rows):
    size = heads * rows
    scale = jnp.exp(later[size:size + heads])[:, None, :]
    memory = scale * unpack(earlier, heads, rows) + unpack(later, heads, rows)
    logs = earlier[size:] + later[size:]
    return jnp.concatenate([memory.reshape(size, -1), logs], axis=0)


def member(position, spots):
    bits = 0
    for spot in spots:
        bits |= 1 << spot
    return ((jnp.int32(bits) >> position) & 1) == 1


def line_rounds(width):
    levels = width.bit_length() - 1
    rounds = []

    def both(pairs):
        fwd = [(s, d, True, True) for s, d in pairs]
        bwd = [(width - 1 - s, width - 1 - d, False, False) for s, d in pairs]
        return fwd + bwd

    for k in range(levels - 1):
        step = 1 << k
        rounds.append(both([(p - step, p) for p in range(2 * step - 1, width, 2 * step)]))
    if width >= 2:
        close = [(0, width - 1, False, True), (width - 1, 0, True, False)]
        if levels >= 2:
            step = width // 4
            close += both([(width // 2 - 1, 3 * step - 1)])
        rounds.append(close)
    for k in range(levels - 3, -1, -1):
        step = 1 << k
        rounds.append(both([(p - step, p) for p in range(3 * step - 1, width, 2 * step)]))
    return rounds


def exclusive_scan(part, axis, lines, width, heads, rows):
    pos = lax.axis_index(axis) % width
    held = part
    before = jnp.zeros_like(part)
    after = part
    for entries in line_rounds(width):
        assert len({e[0] for e in entries}) == len(entries) and len({e[1] for e in entries}) == len(entries)
        send = jnp.where(member(pos, [e[0] for e in entries if e[2]]), held, after)
        full = [(l * width + e[0], l * width + e[1]) for l in range(lines) for e in entries]
        got = lax.ppermute(send, axis, full)
        ahead = jnp.where(member(pos, [e[1] for e in entries if e[3]]), got, 0.0)
        behind = jnp.where(member(pos, [e[1] for e in entries if not e[3]]), got, 0.0)
        held = join(ahead, held, heads, rows)
        before = join(ahead, before, heads, rows)
        after = join(after, behind, heads, rows)
    total = join(before, after, heads, rows)
    if lines == 1:
        return before
    earlier = None
    for shift in range(lines - 1, 0, -1):
        pairs = [((l - shift) * width + p, l * width + p) for l in range(shift, lines) for p in range(width)]
        got = lax.ppermute(total, axis, pairs)
        earlier = got if earlier is None else join(earlier, got, heads, rows)
    return join(earlier, before, heads, rows)


def scatter_heads(partial, axis, n):
    rows, total_cols = partial.shape
    width = total_cols // n
    place = lax.axis_index(axis)
    if n % 2 == 0 and n > 2:
        chips = n // 2
        core = place % 2
        chip = place // 2

        def block(index):
            return lax.dynamic_slice_in_dim(partial, index * width, width, 1)

        keep = jnp.stack([block(2 * y + core) for y in range(chips)])
        away = jnp.stack([block(2 * y + 1 - core) for y in range(chips)])
        pairs = [(h, h ^ 1) for h in range(n)]
        mine = keep + lax.ppermute(away, axis, pairs)
        out = lax.dynamic_index_in_dim(mine, chip, 0, False)
        for shift in sorted(range(1, chips), key=lambda s: (-min(s, chips - s), -s)):
            send = lax.dynamic_index_in_dim(mine, (chip + shift) % chips, 0, False)
            pairs = [(2 * y + c, 2 * ((y + shift) % chips) + c) for y in range(chips) for c in range(2)]
            out = out + lax.ppermute(send, axis, pairs)
        return out
    whole = lax.psum(partial, axis)
    return lax.dynamic_slice_in_dim(whole, place * width, width, 1)


def shards(queries, keys, values, log_decay, norm_gain, out_weight, steer_ids, steer_table, seq_n, seq_width, head_n):
    tok_rows, features = queries.shape
    heads_here = log_decay.shape[1]
    head_size = features // heads_here
    count = tok_rows // SPAN

    def split(array):
        return array.reshape(count, SPAN, heads_here, head_size).transpose(0, 2, 1, 3)

    decays = log_decay.reshape(count, SPAN, heads_here).transpose(0, 2, 1)
    start = jnp.zeros((heads_here, head_size, head_size), jnp.float32)
    def step_with_total(state, inputs):
        new_state, out = block_step(state, inputs)
        return new_state, (out, jnp.cumsum(inputs[3], axis=1)[:, -1])

    local_memory, (blocks, block_logs) = lax.scan(
        step_with_total, start, (split(queries), split(keys), split(values), decays)
    )
    device_log = jnp.sum(block_logs, axis=0)
    lines, width = seq_n // seq_width, seq_width
    passed = exclusive_scan(pack(device_log, local_memory), "seq", lines, width, heads_here, head_size)
    earlier_memory = unpack(passed, heads_here, head_size)
    running = jnp.cumsum(log_decay, axis=0)
    query_heads = queries.reshape(tok_rows, heads_here, head_size).astype(jnp.float32)
    carried = jnp.exp(running)[:, :, None] * jnp.einsum(
        "the,hef->thf", query_heads, earlier_memory, precision=lax.Precision.HIGHEST
    )
    attended = blocks.transpose(0, 2, 1, 3).reshape(tok_rows, heads_here, head_size) + carried
    mean_sq = jnp.mean(attended * attended, axis=-1, keepdims=True)
    normed = (attended * lax.rsqrt(mean_sq + 1e-06)).reshape(tok_rows, features) * norm_gain
    normed = normed.astype(jnp.bfloat16)
    partial_term = lax.optimization_barrier(jnp.dot(normed, out_weight, preferred_element_type=jnp.float32))
    onehot = (
        steer_ids[:, None] == jnp.arange(steer_table.shape[0], dtype=jnp.int32)[None, :]
    ).astype(jnp.bfloat16)
    steering = jnp.dot(onehot, steer_table, preferred_element_type=jnp.float32)
    summed = scatter_heads(partial_term, "head", head_n)
    return (summed + steering).astype(jnp.bfloat16)


def line_width(mesh):
    devices = np.moveaxis(mesh.devices, mesh.axis_names.index("seq"), 0)
    order = devices.reshape(devices.shape[0], -1)[:, 0]
    n = len(order)
    firsts = [tuple(getattr(d, "coords", (0,)))[0] for d in order]
    width = 1
    while width < n and firsts[width] == firsts[0]:
        width += 1
    if n % width or width & (width - 1):
        return n
    return width


def solution(mesh):
    in_specs = (
        P("seq", "head"),
        P("seq", "head"),
        P("seq", "head"),
        P("seq", "head"),
        P("head"),
        P("head", None),
        P("seq"),
        P(None, "head"),
    )
    out_specs = P("seq", "head")
    seq_n = mesh.shape["seq"]
    head_n = mesh.shape["head"]
    seq_width = line_width(mesh)

    def body(*args):
        return shards(*args, seq_n=seq_n, seq_width=seq_width, head_n=head_n)

    return jax.shard_map(body, mesh=mesh, in_specs=in_specs, out_specs=out_specs, check_vma=False)
```

```python
import jax
import jax.numpy as jnp
import numpy as np
from jax import lax
from jax.sharding import PartitionSpec as P

SPAN = 128


def block_step(state, inputs):
    query, key_blk, value_blk, decay = inputs
    cum = jnp.cumsum(decay, axis=1)
    size = decay.shape[1]
    rows = lax.broadcasted_iota(jnp.int32, (size, size), 0)
    cols = lax.broadcasted_iota(jnp.int32, (size, size), 1)
    lower = (cols <= rows)[None]
    scores = jnp.einsum("hte,hse->hts", query, key_blk, preferred_element_type=jnp.float32)
    diffs = jnp.where(lower, cum[:, :, None] - cum[:, None, :], 0.0)
    block_weights = (jnp.where(lower, jnp.exp(diffs), 0.0) * scores).astype(jnp.bfloat16)
    intra = jnp.einsum("hts,hse->hte", block_weights, value_blk, preferred_element_type=jnp.float32)
    inter = jnp.exp(cum)[:, :, None] * jnp.einsum(
        "hte,hef->htf", query.astype(jnp.float32), state, precision=lax.Precision.HIGHEST
    )
    total = cum[:, -1]
    scaled_keys = key_blk.astype(jnp.float32) * jnp.exp(total[:, None] - cum)[:, :, None]
    update = jnp.einsum(
        "hse,hsf->hef", scaled_keys, value_blk.astype(jnp.float32), precision=lax.Precision.HIGHEST
    )
    new_state = jnp.exp(total)[:, None, None] * state + update
    return (new_state, intra + inter)


def pack(log_total, memory):
    heads, rows, cols = memory.shape
    extra = jnp.broadcast_to(log_total[:, None], (heads, cols))
    pad = jnp.zeros(((-heads) % 8, cols), memory.dtype)
    return jnp.concatenate([memory.reshape(heads * rows, cols), extra, pad], axis=0)


def unpack(packed, heads, rows):
    return packed[: heads * rows].reshape(heads, rows, -1)


def join(earlier, later, heads, rows):
    size = heads * rows
    scale = jnp.exp(later[size:size + heads])[:, None, :]
    memory = scale * unpack(earlier, heads, rows) + unpack(later, heads, rows)
    logs = earlier[size:] + later[size:]
    return jnp.concatenate([memory.reshape(size, -1), logs], axis=0)


def member(position, spots):
    bits = 0
    for spot in spots:
        bits |= 1 << spot
    return ((jnp.int32(bits) >> position) & 1) == 1


def line_rounds(width):
    levels = width.bit_length() - 1
    rounds = []

    def both(pairs):
        fwd = [(s, d, True, True) for s, d in pairs]
        bwd = [(width - 1 - s, width - 1 - d, False, False) for s, d in pairs]
        return fwd + bwd

    for k in range(levels - 1):
        step = 1 << k
        rounds.append(both([(p - step, p) for p in range(2 * step - 1, width, 2 * step)]))
    if width >= 2:
        close = [(0, width - 1, False, True), (width - 1, 0, True, False)]
        if levels >= 2:
            step = width // 4
            close += both([(width // 2 - 1, 3 * step - 1)])
        rounds.append(close)
    for k in range(levels - 3, -1, -1):
        step = 1 << k
        rounds.append(both([(p - step, p) for p in range(3 * step - 1, width, 2 * step)]))
    return rounds


def exclusive_scan(part, axis, lines, width, heads, rows):
    pos = lax.axis_index(axis) % width
    held = part
    before = jnp.zeros_like(part)
    after = part
    for entries in line_rounds(width):
        assert len({e[0] for e in entries}) == len(entries) and len({e[1] for e in entries}) == len(entries)
        send = jnp.where(member(pos, [e[0] for e in entries if e[2]]), held, after)
        full = [(l * width + e[0], l * width + e[1]) for l in range(lines) for e in entries]
        got = lax.ppermute(send, axis, full)
        ahead = jnp.where(member(pos, [e[1] for e in entries if e[3]]), got, 0.0)
        behind = jnp.where(member(pos, [e[1] for e in entries if not e[3]]), got, 0.0)
        held = join(ahead, held, heads, rows)
        before = join(ahead, before, heads, rows)
        after = join(after, behind, heads, rows)
    total = join(before, after, heads, rows)
    if lines == 1:
        return before
    earlier = None
    for shift in range(lines - 1, 0, -1):
        pairs = [((l - shift) * width + p, l * width + p) for l in range(shift, lines) for p in range(width)]
        got = lax.ppermute(total, axis, pairs)
        earlier = got if earlier is None else join(earlier, got, heads, rows)
    return join(earlier, before, heads, rows)


def scatter_heads(partial, axis, n):
    rows, total_cols = partial.shape
    width = total_cols // n
    place = lax.axis_index(axis)
    if n % 2 == 0 and n > 2:
        chips = n // 2
        core = place % 2
        chip = place // 2

        def block(index):
            return lax.dynamic_slice_in_dim(partial, index * width, width, 1)

        shifts = sorted(range(1, chips), key=lambda s: -min(s, chips - s))
        pairs = [(h, h ^ 1) for h in range(n)]
        far = shifts[0]
        near = [s for s in range(chips) if s != far]

        def at(shift, parity):
            return block(2 * ((chip + shift) % chips) + parity)

        first = at(far, core) + lax.ppermute(at(far, 1 - core), axis, pairs)
        keep = jnp.stack([at(s, core) for s in near])
        away = jnp.stack([at(s, 1 - core) for s in near])
        rest = keep + lax.ppermute(away, axis, pairs)
        mine = {far: first}
        for i, s in enumerate(near):
            mine[s] = rest[i]
        out = mine[0]
        for shift in shifts:
            send = mine[shift]
            pairs = [(2 * y + c, 2 * ((y + shift) % chips) + c) for y in range(chips) for c in range(2)]
            out = out + lax.ppermute(send, axis, pairs)
        return out
    whole = lax.psum(partial, axis)
    return lax.dynamic_slice_in_dim(whole, place * width, width, 1)


def shards(queries, keys, values, log_decay, norm_gain, out_weight, steer_ids, steer_table, seq_n, seq_width, head_n):
    tok_rows, features = queries.shape
    heads_here = log_decay.shape[1]
    head_size = features // heads_here
    count = tok_rows // SPAN

    def split(array):
        return array.reshape(count, SPAN, heads_here, head_size).transpose(0, 2, 1, 3)

    decays = log_decay.reshape(count, SPAN, heads_here).transpose(0, 2, 1)
    start = jnp.zeros((heads_here, head_size, head_size), jnp.float32)
    def step_with_total(state, inputs):
        new_state, out = block_step(state, inputs)
        return new_state, (out, jnp.cumsum(inputs[3], axis=1)[:, -1])

    local_memory, (blocks, block_logs) = lax.scan(
        step_with_total, start, (split(queries), split(keys), split(values), decays)
    )
    device_log = jnp.sum(block_logs, axis=0)
    lines, width = seq_n // seq_width, seq_width
    passed = exclusive_scan(pack(device_log, local_memory), "seq", lines, width, heads_here, head_size)
    earlier_memory = unpack(passed, heads_here, head_size)
    running = jnp.cumsum(log_decay, axis=0)
    query_heads = queries.reshape(tok_rows, heads_here, head_size).astype(jnp.float32)
    carried = jnp.exp(running)[:, :, None] * jnp.einsum(
        "the,hef->thf", query_heads, earlier_memory, precision=lax.Precision.HIGHEST
    )
    attended = blocks.transpose(0, 2, 1, 3).reshape(tok_rows, heads_here, head_size) + carried
    mean_sq = jnp.mean(attended * attended, axis=-1, keepdims=True)
    normed = (attended * lax.rsqrt(mean_sq + 1e-06)).reshape(tok_rows, features) * norm_gain
    normed = normed.astype(jnp.bfloat16)
    partial_term = lax.optimization_barrier(jnp.dot(normed, out_weight, preferred_element_type=jnp.float32))
    onehot = (
        steer_ids[:, None] == jnp.arange(steer_table.shape[0], dtype=jnp.int32)[None, :]
    ).astype(jnp.bfloat16)
    steering = jnp.dot(onehot, steer_table, preferred_element_type=jnp.float32)
    summed = scatter_heads(partial_term, "head", head_n)
    return (summed + steering).astype(jnp.bfloat16)


def line_width(mesh):
    devices = np.moveaxis(mesh.devices, mesh.axis_names.index("seq"), 0)
    order = devices.reshape(devices.shape[0], -1)[:, 0]
    n = len(order)
    firsts = [tuple(getattr(d, "coords", (0,)))[0] for d in order]
    width = 1
    while width < n and firsts[width] == firsts[0]:
        width += 1
    if n % width or width & (width - 1):
        return n
    return width


def solution(mesh):
    in_specs = (
        P("seq", "head"),
        P("seq", "head"),
        P("seq", "head"),
        P("seq", "head"),
        P("head"),
        P("head", None),
        P("seq"),
        P(None, "head"),
    )
    out_specs = P("seq", "head")
    seq_n = mesh.shape["seq"]
    head_n = mesh.shape["head"]
    seq_width = line_width(mesh)

    def body(*args):
        return shards(*args, seq_n=seq_n, seq_width=seq_width, head_n=head_n)

    return jax.shard_map(body, mesh=mesh, in_specs=in_specs, out_specs=out_specs, check_vma=False)
```
